256 devices in a mesh: pipe: 2 (over core), seq: 32 (over x, z), chan: 4 (over y).
Axes of the slice: x: 4, y: 4, z: 8, core: 2. Of those that a mesh axis runs over, the one named last changes fastest.
Arguments:
- grad_out: bfloat16 [2, 8192, 2048], P('pipe', 'seq', 'chan'), may hold values from -6 to 6
- value_branch: bfloat16 [2, 8192, 2048], P('pipe', 'seq', 'chan'), may hold values from -0.0625 to 0.0625
- key_gate: bfloat16 [2, 8192, 2048], P('pipe', 'seq', 'chan'), may hold values from -6 to 6
- query_gate: bfloat16 [2, 8192, 2048], P('pipe', 'seq', 'chan'), may hold values from -6 to 6
- short_weights: float32 [2, 3, 2048], P('pipe', None, 'chan'), may hold values from -3 to 3
- long_filters: bfloat16 [2, 8192, 2048], P('pipe', 'seq', 'chan'), may hold values from -0.0625 to 0.0625
Outputs:
- passed_grad: bfloat16 [2, 8192, 2048], P('pipe', 'seq', 'chan')
- filter_grad: float32 [2, 8192, 2048], P('pipe', 'seq', 'chan')
The draws below stay inside these ranges and needn't reach their ends.
All inputs are finite; a program needn't handle non-finite values.
Results may differ from the reference program's by a relative error of at most 0.0049.
Values may be sent and summed in bfloat16 or wider, within the bound.
No kernel may reach another device: no remote copies, remote signals or barrier semaphores. Data moves between devices by JAX's collectives and lax.ppermute only.
A program may use at most 64 MiB of HBM per device.

```python
import jax
import jax.numpy as jnp
from jax import lax

CHANNELS = 2048
TOKENS = 8192
SECTIONS = 2


def steps_of(own_key, extent, pieces, smallest, top_value):
    gain = 1.0
    for axis_at, blocks in pieces:
        draws = jax.random.uniform(jax.random.fold_in(jax.random.fold_in(own_key, 6), axis_at), (blocks,), jnp.float32, smallest / len(pieces), top_value / len(pieces))
        gain = gain * jnp.repeat(jnp.exp(draws), extent[axis_at] // blocks).reshape((-1,) + (1,) * (len(extent) - 1 - axis_at))
    return gain


def normal_values(key, dims, spread, reach, shards=(), held_as=jnp.bfloat16):
    entries = jax.random.normal(key, dims, jnp.float32) * spread
    if len(shards) > 0:
        entries = steps_of(key, dims, shards, -0.22, 0.18) * entries
    return jnp.clip(entries, min=-reach, max=reach).astype(held_as)


def setup_inputs(seed: int = 0) -> dict:
    key_of = jax.random.split(jax.random.key(seed), 7)
    return {
        "grad_out": normal_values(key_of[0], (SECTIONS, TOKENS, CHANNELS), 1.0, 6.0, ((0, 2), (1, 32), (2, 4))),
        "value_branch": normal_values(key_of[1], (SECTIONS, TOKENS, CHANNELS), TOKENS ** -0.5, 0.0625, ((0, 2), (1, 32), (2, 4))),
        "key_gate": normal_values(key_of[2], (SECTIONS, TOKENS, CHANNELS), 1.0, 6.0, ((0, 2), (1, 32), (2, 4))),
        "query_gate": normal_values(key_of[3], (SECTIONS, TOKENS, CHANNELS), 1.0, 6.0, ((0, 2), (1, 32), (2, 4))),
        "short_weights": normal_values(key_of[4], (SECTIONS, 3, CHANNELS), 0.5, 3.0, ((0, 2), (2, 4)), jnp.float32),
        "long_filters": normal_values(key_of[5], (SECTIONS, TOKENS, CHANNELS), TOKENS ** -0.5, 0.0625, ((0, 2), (1, 32), (2, 4))),
    }


def one_section(grad_y, value_in, key_in, query_in, weights, filter_in):
    length = grad_y.shape[0]
    padded = 2 * length
    grad_conv = lax.optimization_barrier((query_in.astype(jnp.float32) * grad_y.astype(jnp.float32)).astype(jnp.bfloat16)).astype(jnp.float32)
    gated_value = lax.optimization_barrier((key_in.astype(jnp.float32) * value_in.astype(jnp.float32)).astype(jnp.bfloat16)).astype(jnp.float32)
    spec_conv = jnp.fft.rfft(grad_conv, n=padded, axis=0)
    spec_filter = jnp.fft.rfft(filter_in.astype(jnp.float32), n=padded, axis=0)
    grad_gated = jnp.fft.irfft(spec_conv * jnp.conj(spec_filter), n=padded, axis=0)[:length]
    spec_gated = jnp.fft.rfft(gated_value, n=padded, axis=0)
    filter_grad = jnp.fft.irfft(spec_conv * jnp.conj(spec_gated), n=padded, axis=0)[:length]
    grad_value = key_in.astype(jnp.float32) * grad_gated
    longer = jnp.concatenate([grad_value, jnp.zeros((2, CHANNELS), grad_value.dtype)], axis=0)
    grad_input = weights[0] * longer[:length] + weights[1] * longer[1:length + 1] + weights[2] * longer[2:]
    return grad_input.astype(jnp.bfloat16), filter_grad


def reference(grad_out, value_branch, key_gate, query_gate, short_weights, long_filters):
    inputs_list = []
    filters_list = []
    for section in range(SECTIONS):
        grad_input, filter_grad = one_section(grad_out[section], value_branch[section], key_gate[section], query_gate[section], short_weights[section], long_filters[section])
        inputs_list.append(grad_input)
        filters_list.append(filter_grad)
    passed_grad = jnp.stack([inputs_list[(section + 1) % SECTIONS] for section in range(SECTIONS)])
    return passed_grad, jnp.stack(filters_list)
```

```python
import math

import numpy as np

import jax
import jax.numpy as jnp
from jax import lax
from jax.sharding import PartitionSpec as P

PRECISION = lax.Precision.HIGHEST


def shifted(block, axis, distance):
    devices = range(lax.axis_size(axis))
    route = [((i - distance) % len(devices), i) for i in devices]
    return lax.ppermute(block, axis, route)


def angle_table(first, second, modulus):
    angles = (np.outer(first, second) % modulus) * (2.0 * math.pi / modulus)
    return np.cos(angles), np.sin(angles)


def contract(form, table, values):
    return jnp.einsum(form, jnp.asarray(table, jnp.float32), values, precision=PRECISION)


def forward(signal, padded):
    blocks, _, rows = signal.shape
    half = np.arange(blocks + 1)
    cos_b, sin_b = angle_table(half, np.arange(blocks), 2 * blocks)
    real = contract("ca,akr->ckr", cos_b, signal)
    imag = -contract("ca,akr->ckr", sin_b, signal)
    cos_t, sin_t = angle_table(half, np.arange(rows), padded)
    cos_t = jnp.asarray(cos_t, jnp.float32)[:, None, :]
    sin_t = jnp.asarray(sin_t, jnp.float32)[:, None, :]
    twisted_real = real * cos_t + imag * sin_t
    twisted_imag = imag * cos_t - real * sin_t
    cos_r, sin_r = angle_table(np.arange(rows), np.arange(rows), rows)
    out_real = jnp.einsum("ckr,rd->ckd", twisted_real, jnp.asarray(cos_r, jnp.float32), precision=PRECISION) + jnp.einsum(
        "ckr,rd->ckd", twisted_imag, jnp.asarray(sin_r, jnp.float32), precision=PRECISION
    )
    out_imag = jnp.einsum("ckr,rd->ckd", twisted_imag, jnp.asarray(cos_r, jnp.float32), precision=PRECISION) - jnp.einsum(
        "ckr,rd->ckd", twisted_real, jnp.asarray(sin_r, jnp.float32), precision=PRECISION
    )
    return out_real, out_imag


def inverse(real, imag, padded):
    half_count, _, rows = real.shape
    blocks = half_count - 1
    half = np.arange(half_count)
    cos_r, sin_r = angle_table(np.arange(rows), np.arange(rows), rows)
    cos_r = jnp.asarray(cos_r, jnp.float32)
    sin_r = jnp.asarray(sin_r, jnp.float32)
    back_real = jnp.einsum("ckd,dr->ckr", real, cos_r, precision=PRECISION) - jnp.einsum(
        "ckd,dr->ckr", imag, sin_r, precision=PRECISION
    )
    back_imag = jnp.einsum("ckd,dr->ckr", imag, cos_r, precision=PRECISION) + jnp.einsum(
        "ckd,dr->ckr", real, sin_r, precision=PRECISION
    )
    cos_t, sin_t = angle_table(half, np.arange(rows), padded)
    cos_t = jnp.asarray(cos_t, jnp.float32)[:, None, :]
    sin_t = jnp.asarray(sin_t, jnp.float32)[:, None, :]
    twisted_real = back_real * cos_t - back_imag * sin_t
    twisted_imag = back_imag * cos_t + back_real * sin_t
    weight = np.full(half_count, 2.0)
    weight[0] = 1.0
    weight[blocks] = 1.0
    cos_b, sin_b = angle_table(np.arange(blocks), half, 2 * blocks)
    cos_b = cos_b * weight[None, :] / padded
    sin_b = sin_b * weight[None, :] / padded
    return contract("ac,ckr->akr", cos_b, twisted_real) - contract("ac,ckr->akr", sin_b, twisted_imag)


def body(grad_out, value_branch, key_gate, query_gate, short_weights, long_filters):
    rows, columns = grad_out.shape[1:]
    devices = lax.axis_size("seq")
    position = lax.axis_index("seq")
    group = columns // devices
    padded = 2 * rows * devices
    grad_conv = (query_gate[0].astype(jnp.float32) * grad_out[0].astype(jnp.float32)).astype(jnp.bfloat16)
    gated_value = (key_gate[0].astype(jnp.float32) * value_branch[0].astype(jnp.float32)).astype(jnp.bfloat16)
    stacked = jnp.stack([grad_conv, gated_value, long_filters[0], key_gate[0]])
    send = jnp.swapaxes(stacked, 1, 2).reshape(4, devices, group, rows)
    recv = lax.all_to_all(send, "seq", split_axis=1, concat_axis=1, tiled=True)
    conv_real, conv_imag = forward(recv[0].astype(jnp.float32), padded)
    gated_real, gated_imag = forward(recv[1].astype(jnp.float32), padded)
    filter_real, filter_imag = forward(recv[2].astype(jnp.float32), padded)
    back_real = conv_real * filter_real + conv_imag * filter_imag
    back_imag = conv_imag * filter_real - conv_real * filter_imag
    fold_real = conv_real * gated_real + conv_imag * gated_imag
    fold_imag = conv_imag * gated_real - conv_real * gated_imag
    grad_gated = inverse(back_real, back_imag, padded)
    grad_filter = inverse(fold_real, fold_imag, padded)
    grad_value = recv[3].astype(jnp.float32) * grad_gated
    rim = jnp.concatenate(
        [grad_value[1:, :, :2], jnp.zeros((1, group, 2), grad_value.dtype)], axis=0
    )
    longer = jnp.concatenate([grad_value, rim], axis=2)
    weights = lax.dynamic_slice_in_dim(short_weights[0], position * group, group, axis=1)
    weights = weights[:, None, :, None]
    grad_input = (
        weights[0] * longer[:, :, :rows]
        + weights[1] * longer[:, :, 1 : rows + 1]
        + weights[2] * longer[:, :, 2:]
    ).astype(jnp.bfloat16)
    input_back = lax.all_to_all(grad_input, "seq", split_axis=0, concat_axis=0, tiled=True)
    filter_back = lax.all_to_all(grad_filter, "seq", split_axis=0, concat_axis=0, tiled=True)
    input_tokens = input_back.reshape(columns, rows).T
    filter_tokens = filter_back.reshape(columns, rows).T
    passed = shifted(input_tokens[None], "pipe", -1)
    return (passed, filter_tokens[None])


def solution(mesh):
    placed = (
        P("pipe", "seq", "chan"),
        P("pipe", "seq", "chan"),
        P("pipe", "seq", "chan"),
        P("pipe", "seq", "chan"),
        P("pipe", None, "chan"),
        P("pipe", "seq", "chan"),
    )
    return jax.shard_map(
        body,
        mesh=mesh,
        in_specs=placed,
        out_specs=(P("pipe", "seq", "chan"), P("pipe", "seq", "chan")),
        check_vma=False,
    )
```

```python
import math

import numpy as np

import jax
import jax.numpy as jnp
from jax import lax
from jax.sharding import PartitionSpec as P

PRECISION = lax.Precision.HIGHEST


def shifted(block, axis, distance):
    devices = range(lax.axis_size(axis))
    route = [((i - distance) % len(devices), i) for i in devices]
    return lax.ppermute(block, axis, route)


def angle_table(first, second, modulus):
    angles = (np.outer(first, second) % modulus) * (2.0 * math.pi / modulus)
    return np.cos(angles), np.sin(angles)


def contract(form, table, values):
    return jnp.einsum(form, jnp.asarray(table, jnp.float32), values, precision=PRECISION)


def forward(signal, padded):
    blocks, _, rows = signal.shape
    half = np.arange(blocks + 1)
    cos_b, sin_b = angle_table(half, np.arange(blocks), 2 * blocks)
    real = contract("ca,akr->ckr", cos_b, signal)
    imag = -contract("ca,akr->ckr", sin_b, signal)
    cos_t, sin_t = angle_table(half, np.arange(rows), padded)
    cos_t = jnp.asarray(cos_t, jnp.float32)[:, None, :]
    sin_t = jnp.asarray(sin_t, jnp.float32)[:, None, :]
    twisted_real = real * cos_t + imag * sin_t
    twisted_imag = imag * cos_t - real * sin_t
    cos_r, sin_r = angle_table(np.arange(rows), np.arange(rows), rows)
    out_real = jnp.einsum("ckr,rd->ckd", twisted_real, jnp.asarray(cos_r, jnp.float32), precision=PRECISION) + jnp.einsum(
        "ckr,rd->ckd", twisted_imag, jnp.asarray(sin_r, jnp.float32), precision=PRECISION
    )
    out_imag = jnp.einsum("ckr,rd->ckd", twisted_imag, jnp.asarray(cos_r, jnp.float32), precision=PRECISION) - jnp.einsum(
        "ckr,rd->ckd", twisted_real, jnp.asarray(sin_r, jnp.float32), precision=PRECISION
    )
    return out_real, out_imag


def inverse(real, imag, padded):
    half_count, _, rows = real.shape
    blocks = half_count - 1
    half = np.arange(half_count)
    cos_r, sin_r = angle_table(np.arange(rows), np.arange(rows), rows)
    cos_r = jnp.asarray(cos_r, jnp.float32)
    sin_r = jnp.asarray(sin_r, jnp.float32)
    back_real = jnp.einsum("ckd,dr->ckr", real, cos_r, precision=PRECISION) - jnp.einsum(
        "ckd,dr->ckr", imag, sin_r, precision=PRECISION
    )
    back_imag = jnp.einsum("ckd,dr->ckr", imag, cos_r, precision=PRECISION) + jnp.einsum(
        "ckd,dr->ckr", real, sin_r, precision=PRECISION
    )
    cos_t, sin_t = angle_table(half, np.arange(rows), padded)
    cos_t = jnp.asarray(cos_t, jnp.float32)[:, None, :]
    sin_t = jnp.asarray(sin_t, jnp.float32)[:, None, :]
    twisted_real = back_real * cos_t - back_imag * sin_t
    twisted_imag = back_imag * cos_t + back_real * sin_t
    weight = np.full(half_count, 2.0)
    weight[0] = 1.0
    weight[blocks] = 1.0
    cos_b, sin_b = angle_table(np.arange(blocks), half, 2 * blocks)
    cos_b = cos_b * weight[None, :] / padded
    sin_b = sin_b * weight[None, :] / padded
    return contract("ac,ckr->akr", cos_b, twisted_real) - contract("ac,ckr->akr", sin_b, twisted_imag)


def body(grad_out, value_branch, key_gate, query_gate, short_weights, long_filters):
    rows, columns = grad_out.shape[1:]
    devices = lax.axis_size("seq")
    position = lax.axis_index("seq")
    group = columns // devices
    padded = 2 * rows * devices
    grad_conv = (query_gate[0].astype(jnp.float32) * grad_out[0].astype(jnp.float32)).astype(jnp.bfloat16)
    gated_value = (key_gate[0].astype(jnp.float32) * value_branch[0].astype(jnp.float32)).astype(jnp.bfloat16)
    stacked = jnp.stack([grad_conv, gated_value, long_filters[0], key_gate[0]])
    send = jnp.swapaxes(stacked, 1, 2).reshape(4, devices, group, rows)
    recv = lax.all_to_all(send, "seq", split_axis=1, concat_axis=1, tiled=True)
    conv_real, conv_imag = forward(recv[0].astype(jnp.float32), padded)
    gated_real, gated_imag = forward(recv[1].astype(jnp.float32), padded)
    filter_real, filter_imag = forward(recv[2].astype(jnp.float32), padded)
    back_real = conv_real * filter_real + conv_imag * filter_imag
    back_imag = conv_imag * filter_real - conv_real * filter_imag
    fold_real = conv_real * gated_real + conv_imag * gated_imag
    fold_imag = conv_imag * gated_real - conv_real * gated_imag
    grad_gated = inverse(back_real, back_imag, padded)
    grad_filter = inverse(fold_real, fold_imag, padded)
    grad_value = recv[3].astype(jnp.float32) * grad_gated
    rim = jnp.concatenate(
        [grad_value[1:, :, :2], jnp.zeros((1, group, 2), grad_value.dtype)], axis=0
    )
    longer = jnp.concatenate([grad_value, rim], axis=2)
    weights = lax.dynamic_slice_in_dim(short_weights[0], position * group, group, axis=1)
    weights = weights[:, None, :, None]
    grad_input = (
        weights[0] * longer[:, :, :rows]
        + weights[1] * longer[:, :, 1 : rows + 1]
        + weights[2] * longer[:, :, 2:]
    ).astype(jnp.bfloat16)
    filter_high = lax.reduce_precision(grad_filter, exponent_bits=8, mantissa_bits=7)
    filter_low = grad_filter - filter_high
    outgoing = jnp.stack(
        [grad_input, filter_high.astype(jnp.bfloat16), filter_low.astype(jnp.bfloat16)]
    )
    returned = lax.all_to_all(outgoing, "seq", split_axis=1, concat_axis=1, tiled=True)
    input_tokens = returned[0].reshape(columns, rows).T
    filter_back = returned[1].astype(jnp.float32) + returned[2].astype(jnp.float32)
    filter_tokens = filter_back.reshape(columns, rows).T
    passed = shifted(input_tokens[None], "pipe", -1)
    return (passed, filter_tokens[None])


def solution(mesh):
    placed = (
        P("pipe", "seq", "chan"),
        P("pipe", "seq", "chan"),
        P("pipe", "seq", "chan"),
        P("pipe", "seq", "chan"),
        P("pipe", None, "chan"),
        P("pipe", "seq", "chan"),
    )
    return jax.shard_map(
        body,
        mesh=mesh,
        in_specs=placed,
        out_specs=(P("pipe", "seq", "chan"), P("pipe", "seq", "chan")),
        check_vma=False,
    )
```

```python
import math

import numpy as np

import jax
import jax.numpy as jnp
from jax import lax
from jax.sharding import PartitionSpec as P

PRECISION = lax.Precision.HIGH


def shifted(block, axis, distance):
    devices = range(lax.axis_size(axis))
    route = [((i - distance) % len(devices), i) for i in devices]
    return lax.ppermute(block, axis, route)


def angle_table(first, second, modulus):
    angles = (np.outer(first, second) % modulus) * (2.0 * math.pi / modulus)
    return np.cos(angles), np.sin(angles)


def contract(form, table, values):
    return jnp.einsum(form, jnp.asarray(table, jnp.float32), values, precision=PRECISION)


def forward(signal, padded):
    blocks, _, rows = signal.shape
    half = np.arange(blocks + 1)
    cos_b, sin_b = angle_table(half, np.arange(blocks), 2 * blocks)
    real = contract("ca,akr->ckr", cos_b, signal)
    imag = -contract("ca,akr->ckr", sin_b, signal)
    cos_t, sin_t = angle_table(half, np.arange(rows), padded)
    cos_t = jnp.asarray(cos_t, jnp.float32)[:, None, :]
    sin_t = jnp.asarray(sin_t, jnp.float32)[:, None, :]
    twisted_real = real * cos_t + imag * sin_t
    twisted_imag = imag * cos_t - real * sin_t
    cos_r, sin_r = angle_table(np.arange(rows), np.arange(rows), rows)
    out_real = jnp.einsum("ckr,rd->ckd", twisted_real, jnp.asarray(cos_r, jnp.float32), precision=PRECISION) + jnp.einsum(
        "ckr,rd->ckd", twisted_imag, jnp.asarray(sin_r, jnp.float32), precision=PRECISION
    )
    out_imag = jnp.einsum("ckr,rd->ckd", twisted_imag, jnp.asarray(cos_r, jnp.float32), precision=PRECISION) - jnp.einsum(
        "ckr,rd->ckd", twisted_real, jnp.asarray(sin_r, jnp.float32), precision=PRECISION
    )
    return out_real, out_imag


def inverse(real, imag, padded):
    half_count, _, rows = real.shape
    blocks = half_count - 1
    half = np.arange(half_count)
    cos_r, sin_r = angle_table(np.arange(rows), np.arange(rows), rows)
    cos_r = jnp.asarray(cos_r, jnp.float32)
    sin_r = jnp.asarray(sin_r, jnp.float32)
    back_real = jnp.einsum("ckd,dr->ckr", real, cos_r, precision=PRECISION) - jnp.einsum(
        "ckd,dr->ckr", imag, sin_r, precision=PRECISION
    )
    back_imag = jnp.einsum("ckd,dr->ckr", imag, cos_r, precision=PRECISION) + jnp.einsum(
        "ckd,dr->ckr", real, sin_r, precision=PRECISION
    )
    cos_t, sin_t = angle_table(half, np.arange(rows), padded)
    cos_t = jnp.asarray(cos_t, jnp.float32)[:, None, :]
    sin_t = jnp.asarray(sin_t, jnp.float32)[:, None, :]
    twisted_real = back_real * cos_t - back_imag * sin_t
    twisted_imag = back_imag * cos_t + back_real * sin_t
    weight = np.full(half_count, 2.0)
    weight[0] = 1.0
    weight[blocks] = 1.0
    cos_b, sin_b = angle_table(np.arange(blocks), half, 2 * blocks)
    cos_b = cos_b * weight[None, :] / padded
    sin_b = sin_b * weight[None, :] / padded
    return contract("ac,ckr->akr", cos_b, twisted_real) - contract("ac,ckr->akr", sin_b, twisted_imag)


def body(grad_out, value_branch, key_gate, query_gate, short_weights, long_filters):
    rows, columns = grad_out.shape[1:]
    devices = lax.axis_size("seq")
    position = lax.axis_index("seq")
    group = columns // devices
    padded = 2 * rows * devices
    grad_conv = (query_gate[0].astype(jnp.float32) * grad_out[0].astype(jnp.float32)).astype(jnp.bfloat16)
    gated_value = (key_gate[0].astype(jnp.float32) * value_branch[0].astype(jnp.float32)).astype(jnp.bfloat16)
    stacked = jnp.stack([grad_conv, gated_value, long_filters[0], key_gate[0]])
    send = jnp.swapaxes(stacked, 1, 2).reshape(4, devices, group, rows)
    recv = lax.all_to_all(send, "seq", split_axis=1, concat_axis=1, tiled=True)
    conv_real, conv_imag = forward(recv[0].astype(jnp.float32), padded)
    gated_real, gated_imag = forward(recv[1].astype(jnp.float32), padded)
    filter_real, filter_imag = forward(recv[2].astype(jnp.float32), padded)
    back_real = conv_real * filter_real + conv_imag * filter_imag
    back_imag = conv_imag * filter_real - conv_real * filter_imag
    fold_real = conv_real * gated_real + conv_imag * gated_imag
    fold_imag = conv_imag * gated_real - conv_real * gated_imag
    grad_gated = inverse(back_real, back_imag, padded)
    grad_filter = inverse(fold_real, fold_imag, padded)
    grad_value = recv[3].astype(jnp.float32) * grad_gated
    rim = jnp.concatenate(
        [grad_value[1:, :, :2], jnp.zeros((1, group, 2), grad_value.dtype)], axis=0
    )
    longer = jnp.concatenate([grad_value, rim], axis=2)
    weights = lax.dynamic_slice_in_dim(short_weights[0], position * group, group, axis=1)
    weights = weights[:, None, :, None]
    grad_input = (
        weights[0] * longer[:, :, :rows]
        + weights[1] * longer[:, :, 1 : rows + 1]
        + weights[2] * longer[:, :, 2:]
    ).astype(jnp.bfloat16)
    filter_high = lax.reduce_precision(grad_filter, exponent_bits=8, mantissa_bits=7)
    filter_low = grad_filter - filter_high
    outgoing = jnp.stack(
        [grad_input, filter_high.astype(jnp.bfloat16), filter_low.astype(jnp.bfloat16)]
    )
    returned = lax.all_to_all(outgoing, "seq", split_axis=1, concat_axis=1, tiled=True)
    input_tokens = returned[0].reshape(columns, rows).T
    filter_back = returned[1].astype(jnp.float32) + returned[2].astype(jnp.float32)
    filter_tokens = filter_back.reshape(columns, rows).T
    passed = shifted(input_tokens[None], "pipe", -1)
    return (passed, filter_tokens[None])


def solution(mesh):
    placed = (
        P("pipe", "seq", "chan"),
        P("pipe", "seq", "chan"),
        P("pipe", "seq", "chan"),
        P("pipe", "seq", "chan"),
        P("pipe", None, "chan"),
        P("pipe", "seq", "chan"),
    )
    return jax.shard_map(
        body,
        mesh=mesh,
        in_specs=placed,
        out_specs=(P("pipe", "seq", "chan"), P("pipe", "seq", "chan")),
        check_vma=False,
    )
```

```python
import math

import numpy as np

import jax
import jax.numpy as jnp
from jax import lax
from jax.sharding import PartitionSpec as P

PRECISION = lax.Precision.HIGH


def shifted(block, axis, distance):
    devices = range(lax.axis_size(axis))
    route = [((i - distance) % len(devices), i) for i in devices]
    return lax.ppermute(block, axis, route)


def angle_table(first, second, modulus):
    angles = (np.outer(first, second) % modulus) * (2.0 * math.pi / modulus)
    return np.cos(angles), np.sin(angles)


def contract(form, table, values):
    return jnp.einsum(form, jnp.asarray(table, jnp.float32), values, precision=PRECISION)


def forward(signal, padded):
    blocks, _, rows = signal.shape
    half = np.arange(blocks + 1)
    cos_b, sin_b = angle_table(half, np.arange(blocks), 2 * blocks)
    real = contract("ca,akr->ckr", cos_b, signal)
    imag = -contract("ca,akr->ckr", sin_b, signal)
    cos_t, sin_t = angle_table(half, np.arange(rows), padded)
    cos_t = jnp.asarray(cos_t, jnp.float32)[:, None, :]
    sin_t = jnp.asarray(sin_t, jnp.float32)[:, None, :]
    twisted_real = real * cos_t + imag * sin_t
    twisted_imag = imag * cos_t - real * sin_t
    cos_r, sin_r = angle_table(np.arange(rows), np.arange(rows), rows)
    out_real = jnp.einsum("ckr,rd->ckd", twisted_real, jnp.asarray(cos_r, jnp.float32), precision=PRECISION) + jnp.einsum(
        "ckr,rd->ckd", twisted_imag, jnp.asarray(sin_r, jnp.float32), precision=PRECISION
    )
    out_imag = jnp.einsum("ckr,rd->ckd", twisted_imag, jnp.asarray(cos_r, jnp.float32), precision=PRECISION) - jnp.einsum(
        "ckr,rd->ckd", twisted_real, jnp.asarray(sin_r, jnp.float32), precision=PRECISION
    )
    return out_real, out_imag


def inverse(real, imag, padded):
    half_count, _, rows = real.shape
    blocks = half_count - 1
    half = np.arange(half_count)
    cos_r, sin_r = angle_table(np.arange(rows), np.arange(rows), rows)
    cos_r = jnp.asarray(cos_r, jnp.float32)
    sin_r = jnp.asarray(sin_r, jnp.float32)
    back_real = jnp.einsum("ckd,dr->ckr", real, cos_r, precision=PRECISION) - jnp.einsum(
        "ckd,dr->ckr", imag, sin_r, precision=PRECISION
    )
    back_imag = jnp.einsum("ckd,dr->ckr", imag, cos_r, precision=PRECISION) + jnp.einsum(
        "ckd,dr->ckr", real, sin_r, precision=PRECISION
    )
    cos_t, sin_t = angle_table(half, np.arange(rows), padded)
    cos_t = jnp.asarray(cos_t, jnp.float32)[:, None, :]
    sin_t = jnp.asarray(sin_t, jnp.float32)[:, None, :]
    twisted_real = back_real * cos_t - back_imag * sin_t
    twisted_imag = back_imag * cos_t + back_real * sin_t
    weight = np.full(half_count, 2.0)
    weight[0] = 1.0
    weight[blocks] = 1.0
    cos_b, sin_b = angle_table(np.arange(blocks), half, 2 * blocks)
    cos_b = cos_b * weight[None, :] / padded
    sin_b = sin_b * weight[None, :] / padded
    return contract("ac,ckr->akr", cos_b, twisted_real) - contract("ac,ckr->akr", sin_b, twisted_imag)


def body(grad_out, value_branch, key_gate, query_gate, short_weights, long_filters):
    rows, columns = grad_out.shape[1:]
    devices = lax.axis_size("seq")
    position = lax.axis_index("seq")
    group = columns // devices
    padded = 2 * rows * devices
    grad_conv = (query_gate[0].astype(jnp.float32) * grad_out[0].astype(jnp.float32)).astype(jnp.bfloat16)
    gated_value = (key_gate[0].astype(jnp.float32) * value_branch[0].astype(jnp.float32)).astype(jnp.bfloat16)
    stacked = jnp.stack([grad_conv, gated_value, long_filters[0], key_gate[0]])
    send = jnp.swapaxes(stacked, 1, 2).reshape(4, devices, group, rows)
    recv = lax.all_to_all(send, "seq", split_axis=1, concat_axis=1, tiled=True)
    conv_real, conv_imag = forward(recv[0].astype(jnp.float32), padded)
    gated_real, gated_imag = forward(recv[1].astype(jnp.float32), padded)
    filter_real, filter_imag = forward(recv[2].astype(jnp.float32), padded)
    back_real = conv_real * filter_real + conv_imag * filter_imag
    back_imag = conv_imag * filter_real - conv_real * filter_imag
    fold_real = conv_real * gated_real + conv_imag * gated_imag
    fold_imag = conv_imag * gated_real - conv_real * gated_imag
    grad_gated = inverse(back_real, back_imag, padded)
    grad_filter = inverse(fold_real, fold_imag, padded)
    grad_value = recv[3].astype(jnp.float32) * grad_gated
    rim = jnp.concatenate(
        [grad_value[1:, :, :2], jnp.zeros((1, group, 2), grad_value.dtype)], axis=0
    )
    longer = jnp.concatenate([grad_value, rim], axis=2)
    weights = lax.dynamic_slice_in_dim(short_weights[0], position * group, group, axis=1)
    weights = weights[:, None, :, None]
    grad_input = (
        weights[0] * longer[:, :, :rows]
        + weights[1] * longer[:, :, 1 : rows + 1]
        + weights[2] * longer[:, :, 2:]
    ).astype(jnp.bfloat16)
    outgoing = jnp.stack([grad_input, grad_filter.astype(jnp.bfloat16)])
    returned = lax.all_to_all(outgoing, "seq", split_axis=1, concat_axis=1, tiled=True)
    input_tokens = returned[0].reshape(columns, rows).T
    filter_back = returned[1].astype(jnp.float32)
    filter_tokens = filter_back.reshape(columns, rows).T
    passed = shifted(input_tokens[None], "pipe", -1)
    return (passed, filter_tokens[None])


def solution(mesh):
    placed = (
        P("pipe", "seq", "chan"),
        P("pipe", "seq", "chan"),
        P("pipe", "seq", "chan"),
        P("pipe", "seq", "chan"),
        P("pipe", None, "chan"),
        P("pipe", "seq", "chan"),
    )
    return jax.shard_map(
        body,
        mesh=mesh,
        in_specs=placed,
        out_specs=(P("pipe", "seq", "chan"), P("pipe", "seq", "chan")),
        check_vma=False,
    )
```

```python
import math

import numpy as np

import jax
import jax.numpy as jnp
from jax import lax
from jax.sharding import PartitionSpec as P

PRECISION = lax.Precision.HIGH


def shifted(block, axis, distance):
    devices = range(lax.axis_size(axis))
    route = [((i - distance) % len(devices), i) for i in devices]
    return lax.ppermute(block, axis, route)


def angle_table(first, second, modulus):
    angles = (np.outer(first, second) % modulus) * (2.0 * math.pi / modulus)
    return np.cos(angles), np.sin(angles)


def contract(form, table, values):
    return jnp.einsum(form, jnp.asarray(table, jnp.float32), values, precision=PRECISION)


def forward(signals, padded):
    _, blocks, _, rows = signals.shape
    half = np.arange(blocks + 1)
    cos_b, sin_b = angle_table(half, np.arange(blocks), 2 * blocks)
    first = contract("ja,sakr->sjkr", np.concatenate([cos_b, -sin_b]), signals)
    real, imag = first[:, : blocks + 1], first[:, blocks + 1 :]
    cos_t, sin_t = angle_table(half, np.arange(rows), padded)
    cos_t = jnp.asarray(cos_t, jnp.float32)[:, None, :]
    sin_t = jnp.asarray(sin_t, jnp.float32)[:, None, :]
    twisted = jnp.concatenate([real * cos_t + imag * sin_t, imag * cos_t - real * sin_t], axis=-1)
    cos_r, sin_r = angle_table(np.arange(rows), np.arange(rows), rows)
    table = np.block([[cos_r, -sin_r], [sin_r, cos_r]])
    spectrum = contract("rd,shkr->shkd", table, twisted)
    return spectrum[..., :rows], spectrum[..., rows:]


def inverse(real, imag, padded):
    _, half_count, _, rows = real.shape
    blocks = half_count - 1
    half = np.arange(half_count)
    cos_r, sin_r = angle_table(np.arange(rows), np.arange(rows), rows)
    table = np.block([[cos_r, sin_r], [-sin_r, cos_r]])
    back = contract("dr,shkd->shkr", table, jnp.concatenate([real, imag], axis=-1))
    back_real, back_imag = back[..., :rows], back[..., rows:]
    cos_t, sin_t = angle_table(half, np.arange(rows), padded)
    cos_t = jnp.asarray(cos_t, jnp.float32)[:, None, :]
    sin_t = jnp.asarray(sin_t, jnp.float32)[:, None, :]
    twisted = jnp.concatenate(
        [back_real * cos_t - back_imag * sin_t, back_imag * cos_t + back_real * sin_t], axis=1
    )
    weight = np.full(half_count, 2.0)
    weight[0] = 1.0
    weight[blocks] = 1.0
    cos_b, sin_b = angle_table(np.arange(blocks), half, 2 * blocks)
    table_b = np.concatenate([cos_b, -sin_b], axis=1) * np.concatenate([weight, weight])[None, :] / padded
    return contract("ac,sckr->sakr", table_b, twisted)


def body(grad_out, value_branch, key_gate, query_gate, short_weights, long_filters):
    rows, columns = grad_out.shape[1:]
    devices = lax.axis_size("seq")
    position = lax.axis_index("seq")
    group = columns // devices
    padded = 2 * rows * devices
    grad_conv = (query_gate[0].astype(jnp.float32) * grad_out[0].astype(jnp.float32)).astype(jnp.bfloat16)
    gated_value = (key_gate[0].astype(jnp.float32) * value_branch[0].astype(jnp.float32)).astype(jnp.bfloat16)
    stacked = jnp.stack([grad_conv, gated_value, long_filters[0], key_gate[0]])
    send = jnp.swapaxes(stacked, 1, 2).reshape(4, devices, group, rows)
    recv = lax.all_to_all(send, "seq", split_axis=1, concat_axis=1, tiled=True)
    spec_real, spec_imag = forward(recv[:3].astype(jnp.float32), padded)
    conv_real, conv_imag = spec_real[0], spec_imag[0]
    gated_real, gated_imag = spec_real[1], spec_imag[1]
    filter_real, filter_imag = spec_real[2], spec_imag[2]
    back_real = conv_real * filter_real + conv_imag * filter_imag
    back_imag = conv_imag * filter_real - conv_real * filter_imag
    fold_real = conv_real * gated_real + conv_imag * gated_imag
    fold_imag = conv_imag * gated_real - conv_real * gated_imag
    both = inverse(jnp.stack([back_real, fold_real]), jnp.stack([back_imag, fold_imag]), padded)
    grad_gated, grad_filter = both[0], both[1]
    grad_value = recv[3].astype(jnp.float32) * grad_gated
    rim = jnp.concatenate(
        [grad_value[1:, :, :2], jnp.zeros((1, group, 2), grad_value.dtype)], axis=0
    )
    longer = jnp.concatenate([grad_value, rim], axis=2)
    weights = lax.dynamic_slice_in_dim(short_weights[0], position * group, group, axis=1)
    weights = weights[:, None, :, None]
    grad_input = (
        weights[0] * longer[:, :, :rows]
        + weights[1] * longer[:, :, 1 : rows + 1]
        + weights[2] * longer[:, :, 2:]
    ).astype(jnp.bfloat16)
    outgoing = jnp.stack([grad_input, grad_filter.astype(jnp.bfloat16)])
    returned = lax.all_to_all(outgoing, "seq", split_axis=1, concat_axis=1, tiled=True)
    input_tokens = returned[0].reshape(columns, rows).T
    filter_back = returned[1].astype(jnp.float32)
    filter_tokens = filter_back.reshape(columns, rows).T
    passed = shifted(input_tokens[None], "pipe", -1)
    return (passed, filter_tokens[None])


def solution(mesh):
    placed = (
        P("pipe", "seq", "chan"),
        P("pipe", "seq", "chan"),
        P("pipe", "seq", "chan"),
        P("pipe", "seq", "chan"),
        P("pipe", None, "chan"),
        P("pipe", "seq", "chan"),
    )
    return jax.shard_map(
        body,
        mesh=mesh,
        in_specs=placed,
        out_specs=(P("pipe", "seq", "chan"), P("pipe", "seq", "chan")),
        check_vma=False,
    )
```

```python
import math

import numpy as np

import jax
import jax.numpy as jnp
from jax import lax
from jax.sharding import PartitionSpec as P

PRECISION = lax.Precision.HIGH


def shifted(block, axis, distance):
    devices = range(lax.axis_size(axis))
    route = [((i - distance) % len(devices), i) for i in devices]
    return lax.ppermute(block, axis, route)


def angle_table(first, second, modulus):
    angles = (np.outer(first, second) % modulus) * (2.0 * math.pi / modulus)
    return np.cos(angles), np.sin(angles)


def contract(form, table, values):
    return jnp.einsum(form, jnp.asarray(table, jnp.float32), values, precision=PRECISION)


def forward(signals, padded):
    _, blocks, _, rows = signals.shape
    half = np.arange(blocks + 1)
    cos_b, sin_b = angle_table(half, np.arange(blocks), 2 * blocks)
    first = contract("ja,sakr->sjkr", np.concatenate([cos_b, -sin_b]), signals)
    real, imag = first[:, : blocks + 1], first[:, blocks + 1 :]
    cos_t, sin_t = angle_table(half, np.arange(rows), padded)
    cos_t = jnp.asarray(cos_t, jnp.float32)[:, None, :]
    sin_t = jnp.asarray(sin_t, jnp.float32)[:, None, :]
    twisted = jnp.concatenate([real * cos_t + imag * sin_t, imag * cos_t - real * sin_t], axis=-1)
    cos_r, sin_r = angle_table(np.arange(rows), np.arange(rows), rows)
    table = np.block([[cos_r, -sin_r], [sin_r, cos_r]])
    spectrum = contract("rd,shkr->shkd", table, twisted)
    return spectrum[..., :rows], spectrum[..., rows:]


def inverse(real, imag, padded):
    _, half_count, _, rows = real.shape
    blocks = half_count - 1
    half = np.arange(half_count)
    cos_r, sin_r = angle_table(np.arange(rows), np.arange(rows), rows)
    table = np.block([[cos_r, sin_r], [-sin_r, cos_r]])
    back = contract("dr,shkd->shkr", table, jnp.concatenate([real, imag], axis=-1))
    back_real, back_imag = back[..., :rows], back[..., rows:]
    cos_t, sin_t = angle_table(half, np.arange(rows), padded)
    cos_t = jnp.asarray(cos_t, jnp.float32)[:, None, :]
    sin_t = jnp.asarray(sin_t, jnp.float32)[:, None, :]
    twisted = jnp.concatenate(
        [back_real * cos_t - back_imag * sin_t, back_imag * cos_t + back_real * sin_t], axis=1
    )
    weight = np.full(half_count, 2.0)
    weight[0] = 1.0
    weight[blocks] = 1.0
    cos_b, sin_b = angle_table(np.arange(blocks), half, 2 * blocks)
    table_b = np.concatenate([cos_b, -sin_b], axis=1) * np.concatenate([weight, weight])[None, :] / padded
    return contract("ac,sckr->sakr", table_b, twisted)


def body(grad_out, value_branch, key_gate, query_gate, short_weights, long_filters):
    rows, columns = grad_out.shape[1:]
    devices = lax.axis_size("seq")
    position = lax.axis_index("seq")
    group = columns // devices
    padded = 2 * rows * devices
    grad_conv = (query_gate[0].astype(jnp.float32) * grad_out[0].astype(jnp.float32)).astype(jnp.bfloat16)
    gated_value = (key_gate[0].astype(jnp.float32) * value_branch[0].astype(jnp.float32)).astype(jnp.bfloat16)
    stacked = jnp.stack([grad_conv, gated_value, long_filters[0]])
    send = jnp.swapaxes(stacked, 1, 2).reshape(3, devices, group, rows)
    recv = lax.all_to_all(send, "seq", split_axis=1, concat_axis=1, tiled=True)
    key_send = key_gate[0].T.reshape(devices, group, rows)
    key_recv = lax.all_to_all(key_send, "seq", split_axis=0, concat_axis=0, tiled=True)
    spec_real, spec_imag = forward(recv[:3].astype(jnp.float32), padded)
    conv_real, conv_imag = spec_real[0], spec_imag[0]
    gated_real, gated_imag = spec_real[1], spec_imag[1]
    filter_real, filter_imag = spec_real[2], spec_imag[2]
    back_real = conv_real * filter_real + conv_imag * filter_imag
    back_imag = conv_imag * filter_real - conv_real * filter_imag
    fold_real = conv_real * gated_real + conv_imag * gated_imag
    fold_imag = conv_imag * gated_real - conv_real * gated_imag
    both = inverse(jnp.stack([back_real, fold_real]), jnp.stack([back_imag, fold_imag]), padded)
    grad_gated, grad_filter = both[0], both[1]
    grad_value = key_recv.astype(jnp.float32) * grad_gated
    rim = jnp.concatenate(
        [grad_value[1:, :, :2], jnp.zeros((1, group, 2), grad_value.dtype)], axis=0
    )
    longer = jnp.concatenate([grad_value, rim], axis=2)
    weights = lax.dynamic_slice_in_dim(short_weights[0], position * group, group, axis=1)
    weights = weights[:, None, :, None]
    grad_input = (
        weights[0] * longer[:, :, :rows]
        + weights[1] * longer[:, :, 1 : rows + 1]
        + weights[2] * longer[:, :, 2:]
    ).astype(jnp.bfloat16)
    outgoing = jnp.stack([grad_input, grad_filter.astype(jnp.bfloat16)])
    returned = lax.all_to_all(outgoing, "seq", split_axis=1, concat_axis=1, tiled=True)
    input_tokens = returned[0].reshape(columns, rows).T
    filter_back = returned[1].astype(jnp.float32)
    filter_tokens = filter_back.reshape(columns, rows).T
    passed = shifted(input_tokens[None], "pipe", -1)
    return (passed, filter_tokens[None])


def solution(mesh):
    placed = (
        P("pipe", "seq", "chan"),
        P("pipe", "seq", "chan"),
        P("pipe", "seq", "chan"),
        P("pipe", "seq", "chan"),
        P("pipe", None, "chan"),
        P("pipe", "seq", "chan"),
    )
    return jax.shard_map(
        body,
        mesh=mesh,
        in_specs=placed,
        out_specs=(P("pipe", "seq", "chan"), P("pipe", "seq", "chan")),
        check_vma=False,
    )
```

```python
import math

import numpy as np

import jax
import jax.numpy as jnp
from jax import lax
from jax.sharding import PartitionSpec as P

PRECISION = lax.Precision.HIGH


def shifted(block, axis, distance):
    devices = range(lax.axis_size(axis))
    route = [((i - distance) % len(devices), i) for i in devices]
    return lax.ppermute(block, axis, route)


def angle_table(first, second, modulus):
    angles = (np.outer(first, second) % modulus) * (2.0 * math.pi / modulus)
    return np.cos(angles), np.sin(angles)


def contract(form, table, values):
    return jnp.einsum(form, jnp.asarray(table, jnp.float32), values, precision=PRECISION)


def row_table(rows):
    index = lax.optimization_barrier(jnp.arange(rows, dtype=jnp.int32))
    angles = ((index[:, None] * index[None, :]) % rows).astype(jnp.float32) * (2.0 * math.pi / rows)
    cos_r, sin_r = jnp.cos(angles), jnp.sin(angles)
    return jnp.concatenate(
        [jnp.concatenate([cos_r, -sin_r], axis=1), jnp.concatenate([sin_r, cos_r], axis=1)], axis=0
    )


def forward(signals, table, padded):
    _, blocks, _, rows = signals.shape
    half = np.arange(blocks + 1)
    cos_b, sin_b = angle_table(half, np.arange(blocks), 2 * blocks)
    first = contract("ja,sakr->sjkr", np.concatenate([cos_b, -sin_b]), signals)
    real, imag = first[:, : blocks + 1], first[:, blocks + 1 :]
    cos_t, sin_t = angle_table(half, np.arange(rows), padded)
    cos_t = jnp.asarray(cos_t, jnp.float32)[:, None, :]
    sin_t = jnp.asarray(sin_t, jnp.float32)[:, None, :]
    twisted = jnp.concatenate([real * cos_t + imag * sin_t, imag * cos_t - real * sin_t], axis=-1)
    spectrum = jnp.einsum("rd,shkr->shkd", table, twisted, precision=PRECISION)
    return spectrum[..., :rows], spectrum[..., rows:]


def inverse(real, imag, table, padded):
    _, half_count, _, rows = real.shape
    blocks = half_count - 1
    half = np.arange(half_count)
    back = jnp.einsum(
        "rd,shkd->shkr", table, jnp.concatenate([real, imag], axis=-1), precision=PRECISION
    )
    back_real, back_imag = back[..., :rows], back[..., rows:]
    cos_t, sin_t = angle_table(half, np.arange(rows), padded)
    cos_t = jnp.asarray(cos_t, jnp.float32)[:, None, :]
    sin_t = jnp.asarray(sin_t, jnp.float32)[:, None, :]
    twisted = jnp.concatenate(
        [back_real * cos_t - back_imag * sin_t, back_imag * cos_t + back_real * sin_t], axis=1
    )
    weight = np.full(half_count, 2.0)
    weight[0] = 1.0
    weight[blocks] = 1.0
    cos_b, sin_b = angle_table(np.arange(blocks), half, 2 * blocks)
    table_b = np.concatenate([cos_b, -sin_b], axis=1) * np.concatenate([weight, weight])[None, :] / padded
    return contract("ac,sckr->sakr", table_b, twisted)


def body(grad_out, value_branch, key_gate, query_gate, short_weights, long_filters):
    rows, columns = grad_out.shape[1:]
    devices = lax.axis_size("seq")
    position = lax.axis_index("seq")
    group = columns // devices
    padded = 2 * rows * devices
    grad_conv = (query_gate[0].astype(jnp.float32) * grad_out[0].astype(jnp.float32)).astype(jnp.bfloat16)
    gated_value = (key_gate[0].astype(jnp.float32) * value_branch[0].astype(jnp.float32)).astype(jnp.bfloat16)
    stacked = jnp.stack([grad_conv, gated_value, long_filters[0], key_gate[0]])
    send = jnp.swapaxes(stacked, 1, 2).reshape(4, devices, group, rows)
    recv = lax.all_to_all(send, "seq", split_axis=1, concat_axis=1, tiled=True)
    table = row_table(rows)
    spec_real, spec_imag = forward(recv[:3].astype(jnp.float32), table, padded)
    conv_real, conv_imag = spec_real[0], spec_imag[0]
    gated_real, gated_imag = spec_real[1], spec_imag[1]
    filter_real, filter_imag = spec_real[2], spec_imag[2]
    back_real = conv_real * filter_real + conv_imag * filter_imag
    back_imag = conv_imag * filter_real - conv_real * filter_imag
    fold_real = conv_real * gated_real + conv_imag * gated_imag
    fold_imag = conv_imag * gated_real - conv_real * gated_imag
    both = inverse(jnp.stack([back_real, fold_real]), jnp.stack([back_imag, fold_imag]), table, padded)
    grad_gated, grad_filter = both[0], both[1]
    grad_value = recv[3].astype(jnp.float32) * grad_gated
    rim = jnp.concatenate(
        [grad_value[1:, :, :2], jnp.zeros((1, group, 2), grad_value.dtype)], axis=0
    )
    longer = jnp.concatenate([grad_value, rim], axis=2)
    weights = lax.dynamic_slice_in_dim(short_weights[0], position * group, group, axis=1)
    weights = weights[:, None, :, None]
    grad_input = (
        weights[0] * longer[:, :, :rows]
        + weights[1] * longer[:, :, 1 : rows + 1]
        + weights[2] * longer[:, :, 2:]
    ).astype(jnp.bfloat16)
    outgoing = jnp.stack([grad_input, grad_filter.astype(jnp.bfloat16)])
    returned = lax.all_to_all(outgoing, "seq", split_axis=1, concat_axis=1, tiled=True)
    input_tokens = returned[0].reshape(columns, rows).T
    filter_back = returned[1].astype(jnp.float32)
    filter_tokens = filter_back.reshape(columns, rows).T
    passed = shifted(input_tokens[None], "pipe", -1)
    return (passed, filter_tokens[None])


def solution(mesh):
    placed = (
        P("pipe", "seq", "chan"),
        P("pipe", "seq", "chan"),
        P("pipe", "seq", "chan"),
        P("pipe", "seq", "chan"),
        P("pipe", None, "chan"),
        P("pipe", "seq", "chan"),
    )
    return jax.shard_map(
        body,
        mesh=mesh,
        in_specs=placed,
        out_specs=(P("pipe", "seq", "chan"), P("pipe", "seq", "chan")),
        check_vma=False,
    )
```

```python
import math

import numpy as np

import jax
import jax.numpy as jnp
from jax import lax
from jax.sharding import PartitionSpec as P

PRECISION = lax.Precision.HIGH


def shifted(block, axis, distance):
    devices = range(lax.axis_size(axis))
    route = [((i - distance) % len(devices), i) for i in devices]
    return lax.ppermute(block, axis, route)


def angle_table(first, second, modulus):
    first = lax.optimization_barrier(jnp.asarray(first, jnp.int32))
    products = (first[:, None] * jnp.asarray(second, jnp.int32)[None, :]) % modulus
    angles = products.astype(jnp.float32) * (2.0 * math.pi / modulus)
    return jnp.cos(angles), jnp.sin(angles)


def contract(form, table, values):
    return jnp.einsum(form, jnp.asarray(table, jnp.float32), values, precision=PRECISION)


def row_table(rows):
    index = lax.optimization_barrier(jnp.arange(rows, dtype=jnp.int32))
    angles = ((index[:, None] * index[None, :]) % rows).astype(jnp.float32) * (2.0 * math.pi / rows)
    cos_r, sin_r = jnp.cos(angles), jnp.sin(angles)
    return jnp.concatenate(
        [jnp.concatenate([cos_r, -sin_r], axis=1), jnp.concatenate([sin_r, cos_r], axis=1)], axis=0
    )


def forward(signals, table, padded):
    _, blocks, _, rows = signals.shape
    half = np.arange(blocks + 1)
    cos_b, sin_b = angle_table(half, np.arange(blocks), 2 * blocks)
    first = contract("ja,sakr->sjkr", jnp.concatenate([cos_b, -sin_b]), signals)
    real, imag = first[:, : blocks + 1], first[:, blocks + 1 :]
    cos_t, sin_t = angle_table(half, np.arange(rows), padded)
    cos_t = cos_t[:, None, :]
    sin_t = sin_t[:, None, :]
    twisted = jnp.concatenate([real * cos_t + imag * sin_t, imag * cos_t - real * sin_t], axis=-1)
    spectrum = jnp.einsum("rd,shkr->shkd", table, twisted, precision=PRECISION)
    return spectrum[..., :rows], spectrum[..., rows:]


def inverse(real, imag, table, padded):
    _, half_count, _, rows = real.shape
    blocks = half_count - 1
    half = np.arange(half_count)
    back = jnp.einsum(
        "rd,shkd->shkr", table, jnp.concatenate([real, imag], axis=-1), precision=PRECISION
    )
    back_real, back_imag = back[..., :rows], back[..., rows:]
    cos_t, sin_t = angle_table(half, np.arange(rows), padded)
    cos_t = cos_t[:, None, :]
    sin_t = sin_t[:, None, :]
    twisted = jnp.concatenate(
        [back_real * cos_t - back_imag * sin_t, back_imag * cos_t + back_real * sin_t], axis=1
    )
    weight = np.full(half_count, 2.0)
    weight[0] = 1.0
    weight[blocks] = 1.0
    cos_b, sin_b = angle_table(np.arange(blocks), half, 2 * blocks)
    table_b = jnp.concatenate([cos_b, -sin_b], axis=1) * jnp.asarray(np.concatenate([weight, weight]) / padded, jnp.float32)[None, :]
    return contract("ac,sckr->sakr", table_b, twisted)


def body(grad_out, value_branch, key_gate, query_gate, short_weights, long_filters):
    rows, columns = grad_out.shape[1:]
    devices = lax.axis_size("seq")
    position = lax.axis_index("seq")
    group = columns // devices
    padded = 2 * rows * devices
    grad_conv = (query_gate[0].astype(jnp.float32) * grad_out[0].astype(jnp.float32)).astype(jnp.bfloat16)
    gated_value = (key_gate[0].astype(jnp.float32) * value_branch[0].astype(jnp.float32)).astype(jnp.bfloat16)
    stacked = jnp.stack([grad_conv, gated_value, long_filters[0], key_gate[0]])
    send = jnp.swapaxes(stacked, 1, 2).reshape(4, devices, group, rows)
    recv = lax.all_to_all(send, "seq", split_axis=1, concat_axis=1, tiled=True)
    table = row_table(rows)
    spec_real, spec_imag = forward(recv[:3].astype(jnp.float32), table, padded)
    conv_real, conv_imag = spec_real[0], spec_imag[0]
    gated_real, gated_imag = spec_real[1], spec_imag[1]
    filter_real, filter_imag = spec_real[2], spec_imag[2]
    back_real = conv_real * filter_real + conv_imag * filter_imag
    back_imag = conv_imag * filter_real - conv_real * filter_imag
    fold_real = conv_real * gated_real + conv_imag * gated_imag
    fold_imag = conv_imag * gated_real - conv_real * gated_imag
    both = inverse(jnp.stack([back_real, fold_real]), jnp.stack([back_imag, fold_imag]), table, padded)
    grad_gated, grad_filter = both[0], both[1]
    grad_value = recv[3].astype(jnp.float32) * grad_gated
    rim = jnp.concatenate(
        [grad_value[1:, :, :2], jnp.zeros((1, group, 2), grad_value.dtype)], axis=0
    )
    longer = jnp.concatenate([grad_value, rim], axis=2)
    weights = lax.dynamic_slice_in_dim(short_weights[0], position * group, group, axis=1)
    weights = weights[:, None, :, None]
    grad_input = (
        weights[0] * longer[:, :, :rows]
        + weights[1] * longer[:, :, 1 : rows + 1]
        + weights[2] * longer[:, :, 2:]
    ).astype(jnp.bfloat16)
    outgoing = jnp.stack([grad_input, grad_filter.astype(jnp.bfloat16)])
    returned = lax.all_to_all(outgoing, "seq", split_axis=1, concat_axis=1, tiled=True)
    input_tokens = returned[0].reshape(columns, rows).T
    filter_back = returned[1].astype(jnp.float32)
    filter_tokens = filter_back.reshape(columns, rows).T
    passed = shifted(input_tokens[None], "pipe", -1)
    return (passed, filter_tokens[None])


def solution(mesh):
    placed = (
        P("pipe", "seq", "chan"),
        P("pipe", "seq", "chan"),
        P("pipe", "seq", "chan"),
        P("pipe", "seq", "chan"),
        P("pipe", None, "chan"),
        P("pipe", "seq", "chan"),
    )
    return jax.shard_map(
        body,
        mesh=mesh,
        in_specs=placed,
        out_specs=(P("pipe", "seq", "chan"), P("pipe", "seq", "chan")),
        check_vma=False,
    )
```

```python
import math

import numpy as np

import jax
import jax.numpy as jnp
from jax import lax
from jax.experimental import pallas as pl
from jax.sharding import PartitionSpec as P

PRECISION = lax.Precision.HIGH


def shifted(block, axis, distance):
    devices = range(lax.axis_size(axis))
    route = [((i - distance) % len(devices), i) for i in devices]
    return lax.ppermute(block, axis, route)


def angle_table(first, second, modulus):
    first = lax.optimization_barrier(jnp.asarray(first, jnp.int32))
    products = (first[:, None] * jnp.asarray(second, jnp.int32)[None, :]) % modulus
    angles = products.astype(jnp.float32) * (2.0 * math.pi / modulus)
    return jnp.cos(angles), jnp.sin(angles)


def contract(form, table, values):
    return jnp.einsum(form, jnp.asarray(table, jnp.float32), values, precision=PRECISION)


def row_table(rows):
    index = lax.optimization_barrier(jnp.arange(rows, dtype=jnp.int32))
    angles = ((index[:, None] * index[None, :]) % rows).astype(jnp.float32) * (2.0 * math.pi / rows)
    cos_r, sin_r = jnp.cos(angles), jnp.sin(angles)
    return jnp.concatenate(
        [jnp.concatenate([cos_r, -sin_r], axis=1), jnp.concatenate([sin_r, cos_r], axis=1)], axis=0
    )


def forward(signals, table, padded):
    _, blocks, _, rows = signals.shape
    half = np.arange(blocks + 1)
    cos_b, sin_b = angle_table(half, np.arange(blocks), 2 * blocks)
    first = contract("ja,sakr->sjkr", jnp.concatenate([cos_b, -sin_b]), signals)
    real, imag = first[:, : blocks + 1], first[:, blocks + 1 :]
    cos_t, sin_t = angle_table(half, np.arange(rows), padded)
    cos_t = cos_t[:, None, :]
    sin_t = sin_t[:, None, :]
    twisted = jnp.concatenate([real * cos_t + imag * sin_t, imag * cos_t - real * sin_t], axis=-1)
    spectrum = jnp.einsum("rd,shkr->shkd", table, twisted, precision=PRECISION)
    return spectrum[..., :rows], spectrum[..., rows:]


def inverse(real, imag, table, padded):
    _, half_count, _, rows = real.shape
    blocks = half_count - 1
    half = np.arange(half_count)
    back = jnp.einsum(
        "rd,shkd->shkr", table, jnp.concatenate([real, imag], axis=-1), precision=PRECISION
    )
    back_real, back_imag = back[..., :rows], back[..., rows:]
    cos_t, sin_t = angle_table(half, np.arange(rows), padded)
    cos_t = cos_t[:, None, :]
    sin_t = sin_t[:, None, :]
    twisted = jnp.concatenate(
        [back_real * cos_t - back_imag * sin_t, back_imag * cos_t + back_real * sin_t], axis=1
    )
    weight = np.full(half_count, 2.0)
    weight[0] = 1.0
    weight[blocks] = 1.0
    cos_b, sin_b = angle_table(np.arange(blocks), half, 2 * blocks)
    table_b = jnp.concatenate([cos_b, -sin_b], axis=1) * jnp.asarray(np.concatenate([weight, weight]) / padded, jnp.float32)[None, :]
    return contract("ac,sckr->sakr", table_b, twisted)


def prep_kernel(grad_ref, value_ref, key_ref, query_ref, filter_ref, out_ref):
    key = key_ref[...].astype(jnp.float32)
    grad_conv = (query_ref[...].astype(jnp.float32) * grad_ref[...].astype(jnp.float32)).astype(jnp.bfloat16)
    gated_value = (key * value_ref[...].astype(jnp.float32)).astype(jnp.bfloat16)
    devices, _, group, rows = out_ref.shape
    for index, block in enumerate([grad_conv, gated_value, filter_ref[...], key_ref[...]]):
        flipped = block.astype(jnp.float32).T.reshape(devices, group, rows)
        out_ref[:, index] = flipped.astype(jnp.bfloat16)


def body(grad_out, value_branch, key_gate, query_gate, short_weights, long_filters):
    rows, columns = grad_out.shape[1:]
    devices = lax.axis_size("seq")
    position = lax.axis_index("seq")
    group = columns // devices
    padded = 2 * rows * devices
    send = pl.pallas_call(
        prep_kernel, out_shape=jax.ShapeDtypeStruct((devices, 4, group, rows), jnp.bfloat16)
    )(grad_out[0], value_branch[0], key_gate[0], query_gate[0], long_filters[0])
    recv = lax.all_to_all(send, "seq", split_axis=0, concat_axis=0, tiled=True)
    table = row_table(rows)
    spec_real, spec_imag = forward(jnp.swapaxes(recv[:, :3], 0, 1).astype(jnp.float32), table, padded)
    conv_real, conv_imag = spec_real[0], spec_imag[0]
    gated_real, gated_imag = spec_real[1], spec_imag[1]
    filter_real, filter_imag = spec_real[2], spec_imag[2]
    back_real = conv_real * filter_real + conv_imag * filter_imag
    back_imag = conv_imag * filter_real - conv_real * filter_imag
    fold_real = conv_real * gated_real + conv_imag * gated_imag
    fold_imag = conv_imag * gated_real - conv_real * gated_imag
    both = inverse(jnp.stack([back_real, fold_real]), jnp.stack([back_imag, fold_imag]), table, padded)
    grad_gated, grad_filter = both[0], both[1]
    grad_value = recv[:, 3].astype(jnp.float32) * grad_gated
    rim = jnp.concatenate(
        [grad_value[1:, :, :2], jnp.zeros((1, group, 2), grad_value.dtype)], axis=0
    )
    longer = jnp.concatenate([grad_value, rim], axis=2)
    weights = lax.dynamic_slice_in_dim(short_weights[0], position * group, group, axis=1)
    weights = weights[:, None, :, None]
    grad_input = (
        weights[0] * longer[:, :, :rows]
        + weights[1] * longer[:, :, 1 : rows + 1]
        + weights[2] * longer[:, :, 2:]
    ).astype(jnp.bfloat16)
    outgoing = jnp.stack([grad_input, grad_filter.astype(jnp.bfloat16)])
    returned = lax.all_to_all(outgoing, "seq", split_axis=1, concat_axis=1, tiled=True)
    input_tokens = returned[0].reshape(columns, rows).T
    filter_back = returned[1].astype(jnp.float32)
    filter_tokens = filter_back.reshape(columns, rows).T
    passed = shifted(input_tokens[None], "pipe", -1)
    return (passed, filter_tokens[None])


def solution(mesh):
    placed = (
        P("pipe", "seq", "chan"),
        P("pipe", "seq", "chan"),
        P("pipe", "seq", "chan"),
        P("pipe", "seq", "chan"),
        P("pipe", None, "chan"),
        P("pipe", "seq", "chan"),
    )
    return jax.shard_map(
        body,
        mesh=mesh,
        in_specs=placed,
        out_specs=(P("pipe", "seq", "chan"), P("pipe", "seq", "chan")),
        check_vma=False,
    )
```

```python
import math

import numpy as np

import jax
import jax.numpy as jnp
from jax import lax
from jax.experimental import pallas as pl
from jax.sharding import PartitionSpec as P

PRECISION = lax.Precision.HIGH


def shifted(block, axis, distance):
    devices = range(lax.axis_size(axis))
    route = [((i - distance) % len(devices), i) for i in devices]
    return lax.ppermute(block, axis, route)


def angle_table(first, second, modulus):
    first = lax.optimization_barrier(jnp.asarray(first, jnp.int32))
    products = (first[:, None] * jnp.asarray(second, jnp.int32)[None, :]) % modulus
    angles = products.astype(jnp.float32) * (2.0 * math.pi / modulus)
    return jnp.cos(angles), jnp.sin(angles)


def contract(form, table, values):
    return jnp.einsum(form, jnp.asarray(table, jnp.float32), values, precision=PRECISION)


def row_table(rows):
    index = lax.optimization_barrier(jnp.arange(rows, dtype=jnp.int32))
    angles = ((index[:, None] * index[None, :]) % rows).astype(jnp.float32) * (2.0 * math.pi / rows)
    cos_r, sin_r = jnp.cos(angles), jnp.sin(angles)
    return jnp.concatenate(
        [jnp.concatenate([cos_r, -sin_r], axis=1), jnp.concatenate([sin_r, cos_r], axis=1)], axis=0
    )


def forward(signals, table, padded):
    _, blocks, _, rows = signals.shape
    half = np.arange(blocks + 1)
    cos_b, sin_b = angle_table(half, np.arange(blocks), 2 * blocks)
    first = contract("ja,sakr->sjkr", jnp.concatenate([cos_b, -sin_b]), signals)
    real, imag = first[:, : blocks + 1], first[:, blocks + 1 :]
    cos_t, sin_t = angle_table(half, np.arange(rows), padded)
    cos_t = cos_t[:, None, :]
    sin_t = sin_t[:, None, :]
    twisted = jnp.concatenate([real * cos_t + imag * sin_t, imag * cos_t - real * sin_t], axis=-1)
    spectrum = jnp.einsum("rd,shkr->shkd", table, twisted, precision=PRECISION)
    return spectrum[..., :rows], spectrum[..., rows:]


def inverse(real, imag, table, padded):
    _, half_count, _, rows = real.shape
    blocks = half_count - 1
    half = np.arange(half_count)
    back = jnp.einsum(
        "rd,shkd->shkr", table, jnp.concatenate([real, imag], axis=-1), precision=PRECISION
    )
    back_real, back_imag = back[..., :rows], back[..., rows:]
    cos_t, sin_t = angle_table(half, np.arange(rows), padded)
    cos_t = cos_t[:, None, :]
    sin_t = sin_t[:, None, :]
    twisted = jnp.concatenate(
        [back_real * cos_t - back_imag * sin_t, back_imag * cos_t + back_real * sin_t], axis=1
    )
    weight = np.full(half_count, 2.0)
    weight[0] = 1.0
    weight[blocks] = 1.0
    cos_b, sin_b = angle_table(np.arange(blocks), half, 2 * blocks)
    table_b = jnp.concatenate([cos_b, -sin_b], axis=1) * jnp.asarray(np.concatenate([weight, weight]) / padded, jnp.float32)[None, :]
    return contract("ac,sckr->askr", table_b, twisted)


def prep_kernel(grad_ref, value_ref, key_ref, query_ref, filter_ref, out_ref):
    key = key_ref[...].astype(jnp.float32)
    grad_conv = (query_ref[...].astype(jnp.float32) * grad_ref[...].astype(jnp.float32)).astype(jnp.bfloat16)
    gated_value = (key * value_ref[...].astype(jnp.float32)).astype(jnp.bfloat16)
    devices, _, group, rows = out_ref.shape
    for index, block in enumerate([grad_conv, gated_value, filter_ref[...], key_ref[...]]):
        flipped = block.astype(jnp.float32).T.reshape(devices, group, rows)
        out_ref[:, index] = flipped.astype(jnp.bfloat16)


def body(grad_out, value_branch, key_gate, query_gate, short_weights, long_filters):
    rows, columns = grad_out.shape[1:]
    devices = lax.axis_size("seq")
    position = lax.axis_index("seq")
    group = columns // devices
    padded = 2 * rows * devices
    send = pl.pallas_call(
        prep_kernel, out_shape=jax.ShapeDtypeStruct((devices, 4, group, rows), jnp.bfloat16)
    )(grad_out[0], value_branch[0], key_gate[0], query_gate[0], long_filters[0])
    recv = lax.all_to_all(send, "seq", split_axis=0, concat_axis=0, tiled=True)
    table = row_table(rows)
    spec_real, spec_imag = forward(jnp.swapaxes(recv[:, :3], 0, 1).astype(jnp.float32), table, padded)
    conv_real, conv_imag = spec_real[0], spec_imag[0]
    gated_real, gated_imag = spec_real[1], spec_imag[1]
    filter_real, filter_imag = spec_real[2], spec_imag[2]
    back_real = conv_real * filter_real + conv_imag * filter_imag
    back_imag = conv_imag * filter_real - conv_real * filter_imag
    fold_real = conv_real * gated_real + conv_imag * gated_imag
    fold_imag = conv_imag * gated_real - conv_real * gated_imag
    both = inverse(jnp.stack([back_real, fold_real]), jnp.stack([back_imag, fold_imag]), table, padded)
    grad_gated, grad_filter = both[:, 0], both[:, 1]
    grad_value = recv[:, 3].astype(jnp.float32) * grad_gated
    rim = jnp.concatenate(
        [grad_value[1:, :, :2], jnp.zeros((1, group, 2), grad_value.dtype)], axis=0
    )
    longer = jnp.concatenate([grad_value, rim], axis=2)
    weights = lax.dynamic_slice_in_dim(short_weights[0], position * group, group, axis=1)
    weights = weights[:, None, :, None]
    grad_input = (
        weights[0] * longer[:, :, :rows]
        + weights[1] * longer[:, :, 1 : rows + 1]
        + weights[2] * longer[:, :, 2:]
    ).astype(jnp.bfloat16)
    outgoing = jnp.stack([grad_input, grad_filter.astype(jnp.bfloat16)])
    returned = lax.all_to_all(outgoing, "seq", split_axis=1, concat_axis=1, tiled=True)
    input_tokens = returned[0].reshape(columns, rows).T
    filter_back = returned[1].astype(jnp.float32)
    filter_tokens = filter_back.reshape(columns, rows).T
    passed = shifted(input_tokens[None], "pipe", -1)
    return (passed, filter_tokens[None])


def solution(mesh):
    placed = (
        P("pipe", "seq", "chan"),
        P("pipe", "seq", "chan"),
        P("pipe", "seq", "chan"),
        P("pipe", "seq", "chan"),
        P("pipe", None, "chan"),
        P("pipe", "seq", "chan"),
    )
    return jax.shard_map(
        body,
        mesh=mesh,
        in_specs=placed,
        out_specs=(P("pipe", "seq", "chan"), P("pipe", "seq", "chan")),
        check_vma=False,
    )
```

```python
import math

import numpy as np

import jax
import jax.numpy as jnp
from jax import lax
from jax.experimental import pallas as pl
from jax.sharding import PartitionSpec as P

PRECISION = lax.Precision.HIGH


def shifted(block, axis, distance):
    devices = range(lax.axis_size(axis))
    route = [((i - distance) % len(devices), i) for i in devices]
    return lax.ppermute(block, axis, route)


def angle_table(first, second, modulus):
    first = lax.optimization_barrier(jnp.asarray(first, jnp.int32))
    products = (first[:, None] * jnp.asarray(second, jnp.int32)[None, :]) % modulus
    angles = products.astype(jnp.float32) * (2.0 * math.pi / modulus)
    return jnp.cos(angles), jnp.sin(angles)


def contract(form, table, values):
    return jnp.einsum(form, jnp.asarray(table, jnp.float32), values, precision=PRECISION)


def row_table(rows):
    index = lax.optimization_barrier(jnp.arange(rows, dtype=jnp.int32))
    angles = ((index[:, None] * index[None, :]) % rows).astype(jnp.float32) * (2.0 * math.pi / rows)
    cos_r, sin_r = jnp.cos(angles), jnp.sin(angles)
    return jnp.concatenate(
        [jnp.concatenate([cos_r, -sin_r], axis=1), jnp.concatenate([sin_r, cos_r], axis=1)], axis=0
    )


def forward(signals, table, padded):
    _, blocks, _, rows = signals.shape
    half = np.arange(blocks + 1)
    cos_b, sin_b = angle_table(half, np.arange(blocks), 2 * blocks)
    first = contract("ja,sakr->sjkr", jnp.concatenate([cos_b, -sin_b]), signals)
    real, imag = first[:, : blocks + 1], first[:, blocks + 1 :]
    cos_t, sin_t = angle_table(half, np.arange(rows), padded)
    cos_t = cos_t[:, None, :]
    sin_t = sin_t[:, None, :]
    twisted = jnp.concatenate([real * cos_t + imag * sin_t, imag * cos_t - real * sin_t], axis=-1)
    spectrum = jnp.einsum("rd,shkr->shkd", table, twisted, precision=PRECISION)
    return spectrum[..., :rows], spectrum[..., rows:]


def inverse(real, imag, table, padded):
    _, half_count, _, rows = real.shape
    blocks = half_count - 1
    half = np.arange(half_count)
    back = jnp.einsum(
        "rd,shkd->shkr", table, jnp.concatenate([real, imag], axis=-1), precision=PRECISION
    )
    back_real, back_imag = back[..., :rows], back[..., rows:]
    cos_t, sin_t = angle_table(half, np.arange(rows), padded)
    cos_t = cos_t[:, None, :]
    sin_t = sin_t[:, None, :]
    twisted = jnp.concatenate(
        [back_real * cos_t - back_imag * sin_t, back_imag * cos_t + back_real * sin_t], axis=1
    )
    weight = np.full(half_count, 2.0)
    weight[0] = 1.0
    weight[blocks] = 1.0
    cos_b, sin_b = angle_table(np.arange(blocks), half, 2 * blocks)
    table_b = jnp.concatenate([cos_b, -sin_b], axis=1) * jnp.asarray(np.concatenate([weight, weight]) / padded, jnp.float32)[None, :]
    return contract("ac,sckr->askr", table_b, twisted)


def prep_kernel(grad_ref, value_ref, key_ref, query_ref, filter_ref, out_ref):
    key = key_ref[...].astype(jnp.float32)
    grad_conv = (query_ref[...].astype(jnp.float32) * grad_ref[...].astype(jnp.float32)).astype(jnp.bfloat16)
    gated_value = (key * value_ref[...].astype(jnp.float32)).astype(jnp.bfloat16)
    devices, _, group, rows = out_ref.shape
    for index, block in enumerate([grad_conv, gated_value, filter_ref[...], key_ref[...]]):
        flipped = block.astype(jnp.float32).T.reshape(devices, group, rows)
        out_ref[:, index] = flipped.astype(jnp.bfloat16)


def tail_kernel(returned_ref, input_ref, filter_ref):
    _, devices, group, rows = returned_ref.shape
    for index, out_ref in enumerate([input_ref, filter_ref]):
        block = returned_ref[index].astype(jnp.float32).reshape(devices * group, rows)
        out_ref[...] = block.T.astype(out_ref.dtype)


def body(grad_out, value_branch, key_gate, query_gate, short_weights, long_filters):
    rows, columns = grad_out.shape[1:]
    devices = lax.axis_size("seq")
    position = lax.axis_index("seq")
    group = columns // devices
    padded = 2 * rows * devices
    send = pl.pallas_call(
        prep_kernel, out_shape=jax.ShapeDtypeStruct((devices, 4, group, rows), jnp.bfloat16)
    )(grad_out[0], value_branch[0], key_gate[0], query_gate[0], long_filters[0])
    recv = lax.all_to_all(send, "seq", split_axis=0, concat_axis=0, tiled=True)
    table = row_table(rows)
    spec_real, spec_imag = forward(jnp.swapaxes(recv[:, :3], 0, 1).astype(jnp.float32), table, padded)
    conv_real, conv_imag = spec_real[0], spec_imag[0]
    gated_real, gated_imag = spec_real[1], spec_imag[1]
    filter_real, filter_imag = spec_real[2], spec_imag[2]
    back_real = conv_real * filter_real + conv_imag * filter_imag
    back_imag = conv_imag * filter_real - conv_real * filter_imag
    fold_real = conv_real * gated_real + conv_imag * gated_imag
    fold_imag = conv_imag * gated_real - conv_real * gated_imag
    both = inverse(jnp.stack([back_real, fold_real]), jnp.stack([back_imag, fold_imag]), table, padded)
    grad_gated, grad_filter = both[:, 0], both[:, 1]
    grad_value = recv[:, 3].astype(jnp.float32) * grad_gated
    rim = jnp.concatenate(
        [grad_value[1:, :, :2], jnp.zeros((1, group, 2), grad_value.dtype)], axis=0
    )
    longer = jnp.concatenate([grad_value, rim], axis=2)
    weights = lax.dynamic_slice_in_dim(short_weights[0], position * group, group, axis=1)
    weights = weights[:, None, :, None]
    grad_input = (
        weights[0] * longer[:, :, :rows]
        + weights[1] * longer[:, :, 1 : rows + 1]
        + weights[2] * longer[:, :, 2:]
    ).astype(jnp.bfloat16)
    outgoing = jnp.stack([grad_input, grad_filter.astype(jnp.bfloat16)])
    returned = lax.all_to_all(outgoing, "seq", split_axis=1, concat_axis=1, tiled=True)
    input_tokens, filter_tokens = pl.pallas_call(
        tail_kernel,
        out_shape=(
            jax.ShapeDtypeStruct((rows, columns), jnp.bfloat16),
            jax.ShapeDtypeStruct((rows, columns), jnp.float32),
        ),
    )(returned)
    passed = shifted(input_tokens[None], "pipe", -1)
    return (passed, filter_tokens[None])


def solution(mesh):
    placed = (
        P("pipe", "seq", "chan"),
        P("pipe", "seq", "chan"),
        P("pipe", "seq", "chan"),
        P("pipe", "seq", "chan"),
        P("pipe", None, "chan"),
        P("pipe", "seq", "chan"),
    )
    return jax.shard_map(
        body,
        mesh=mesh,
        in_specs=placed,
        out_specs=(P("pipe", "seq", "chan"), P("pipe", "seq", "chan")),
        check_vma=False,
    )
```

```python
import math

import numpy as np

import jax
import jax.numpy as jnp
from jax import lax
from jax.experimental import pallas as pl
from jax.sharding import PartitionSpec as P

PRECISION = lax.Precision.HIGH


def shifted(block, axis, distance):
    devices = range(lax.axis_size(axis))
    route = [((i - distance) % len(devices), i) for i in devices]
    return lax.ppermute(block, axis, route)


def angle_table(first, second, modulus):
    first = lax.optimization_barrier(jnp.asarray(first, jnp.int32))
    products = (first[:, None] * jnp.asarray(second, jnp.int32)[None, :]) % modulus
    angles = products.astype(jnp.float32) * (2.0 * math.pi / modulus)
    return jnp.cos(angles), jnp.sin(angles)


def contract(form, table, values):
    return jnp.einsum(form, jnp.asarray(table, jnp.float32), values, precision=PRECISION)


def row_table(rows):
    index = lax.optimization_barrier(jnp.arange(rows, dtype=jnp.int32))
    angles = ((index[:, None] * index[None, :]) % rows).astype(jnp.float32) * (2.0 * math.pi / rows)
    cos_r, sin_r = jnp.cos(angles), jnp.sin(angles)
    return jnp.concatenate(
        [jnp.concatenate([cos_r, -sin_r], axis=1), jnp.concatenate([sin_r, cos_r], axis=1)], axis=0
    )


def forward(signals, table, padded):
    _, blocks, _, rows = signals.shape
    half = np.arange(blocks + 1)
    cos_b, sin_b = angle_table(half, np.arange(blocks), 2 * blocks)
    first = contract("ja,sakr->sjkr", jnp.concatenate([cos_b, -sin_b]), signals)
    real, imag = first[:, : blocks + 1], first[:, blocks + 1 :]
    cos_t, sin_t = angle_table(half, np.arange(rows), padded)
    cos_t = cos_t[:, None, :]
    sin_t = sin_t[:, None, :]
    twisted = jnp.concatenate([real * cos_t + imag * sin_t, imag * cos_t - real * sin_t], axis=-1)
    spectrum = jnp.einsum("rd,shkr->shkd", table, twisted, precision=PRECISION)
    return spectrum[..., :rows], spectrum[..., rows:]


def inverse(real, imag, table, padded):
    _, half_count, _, rows = real.shape
    blocks = half_count - 1
    half = np.arange(half_count)
    back = jnp.einsum(
        "rd,shkd->shkr", table, jnp.concatenate([real, imag], axis=-1), precision=PRECISION
    )
    back_real, back_imag = back[..., :rows], back[..., rows:]
    cos_t, sin_t = angle_table(half, np.arange(rows), padded)
    cos_t = cos_t[:, None, :]
    sin_t = sin_t[:, None, :]
    twisted = jnp.concatenate(
        [back_real * cos_t - back_imag * sin_t, back_imag * cos_t + back_real * sin_t], axis=1
    )
    weight = np.full(half_count, 2.0)
    weight[0] = 1.0
    weight[blocks] = 1.0
    cos_b, sin_b = angle_table(np.arange(blocks), half, 2 * blocks)
    table_b = jnp.concatenate([cos_b, -sin_b], axis=1) * jnp.asarray(np.concatenate([weight, weight]) / padded, jnp.float32)[None, :]
    return contract("ac,sckr->askr", table_b, twisted)


def prep_kernel(grad_ref, value_ref, key_ref, query_ref, filter_ref, out_ref):
    key = key_ref[...].astype(jnp.float32)
    grad_conv = (query_ref[...].astype(jnp.float32) * grad_ref[...].astype(jnp.float32)).astype(jnp.bfloat16)
    gated_value = (key * value_ref[...].astype(jnp.float32)).astype(jnp.bfloat16)
    devices, _, group, rows = out_ref.shape
    for index, block in enumerate([grad_conv, gated_value, filter_ref[...], key_ref[...]]):
        out_ref[:, index] = block.T.reshape(devices, group, rows)


def body(grad_out, value_branch, key_gate, query_gate, short_weights, long_filters):
    rows, columns = grad_out.shape[1:]
    devices = lax.axis_size("seq")
    position = lax.axis_index("seq")
    group = columns // devices
    padded = 2 * rows * devices
    send = pl.pallas_call(
        prep_kernel, out_shape=jax.ShapeDtypeStruct((devices, 4, group, rows), jnp.bfloat16)
    )(grad_out[0], value_branch[0], key_gate[0], query_gate[0], long_filters[0])
    recv = lax.all_to_all(send, "seq", split_axis=0, concat_axis=0, tiled=True)
    table = row_table(rows)
    spec_real, spec_imag = forward(jnp.swapaxes(recv[:, :3], 0, 1).astype(jnp.float32), table, padded)
    conv_real, conv_imag = spec_real[0], spec_imag[0]
    gated_real, gated_imag = spec_real[1], spec_imag[1]
    filter_real, filter_imag = spec_real[2], spec_imag[2]
    back_real = conv_real * filter_real + conv_imag * filter_imag
    back_imag = conv_imag * filter_real - conv_real * filter_imag
    fold_real = conv_real * gated_real + conv_imag * gated_imag
    fold_imag = conv_imag * gated_real - conv_real * gated_imag
    both = inverse(jnp.stack([back_real, fold_real]), jnp.stack([back_imag, fold_imag]), table, padded)
    grad_gated, grad_filter = both[:, 0], both[:, 1]
    grad_value = recv[:, 3].astype(jnp.float32) * grad_gated
    rim = jnp.concatenate(
        [grad_value[1:, :, :2], jnp.zeros((1, group, 2), grad_value.dtype)], axis=0
    )
    longer = jnp.concatenate([grad_value, rim], axis=2)
    weights = lax.dynamic_slice_in_dim(short_weights[0], position * group, group, axis=1)
    weights = weights[:, None, :, None]
    grad_input = (
        weights[0] * longer[:, :, :rows]
        + weights[1] * longer[:, :, 1 : rows + 1]
        + weights[2] * longer[:, :, 2:]
    ).astype(jnp.bfloat16)
    outgoing = jnp.stack([grad_input, grad_filter.astype(jnp.bfloat16)])
    returned = lax.all_to_all(outgoing, "seq", split_axis=1, concat_axis=1, tiled=True)
    input_tokens = returned[0].reshape(columns, rows).T
    filter_back = returned[1].astype(jnp.float32)
    filter_tokens = filter_back.reshape(columns, rows).T
    passed = shifted(input_tokens[None], "pipe", -1)
    return (passed, filter_tokens[None])


def solution(mesh):
    placed = (
        P("pipe", "seq", "chan"),
        P("pipe", "seq", "chan"),
        P("pipe", "seq", "chan"),
        P("pipe", "seq", "chan"),
        P("pipe", None, "chan"),
        P("pipe", "seq", "chan"),
    )
    return jax.shard_map(
        body,
        mesh=mesh,
        in_specs=placed,
        out_specs=(P("pipe", "seq", "chan"), P("pipe", "seq", "chan")),
        check_vma=False,
    )
```

```python
import math

import numpy as np

import jax
import jax.numpy as jnp
from jax import lax
from jax.experimental import pallas as pl
from jax.sharding import PartitionSpec as P

PRECISION = lax.Precision.HIGH


def shifted(block, axis, distance):
    devices = range(lax.axis_size(axis))
    route = [((i - distance) % len(devices), i) for i in devices]
    return lax.ppermute(block, axis, route)


def angle_table(first, second, modulus):
    first = lax.optimization_barrier(jnp.asarray(first, jnp.int32))
    products = (first[:, None] * jnp.asarray(second, jnp.int32)[None, :]) % modulus
    angles = products.astype(jnp.float32) * (2.0 * math.pi / modulus)
    return jnp.cos(angles), jnp.sin(angles)


def contract(form, table, values):
    return jnp.einsum(form, jnp.asarray(table, jnp.float32), values, precision=PRECISION)


def row_table(rows):
    index = lax.optimization_barrier(jnp.arange(rows, dtype=jnp.int32))
    angles = ((index[:, None] * index[None, :]) % rows).astype(jnp.float32) * (2.0 * math.pi / rows)
    cos_r, sin_r = jnp.cos(angles), jnp.sin(angles)
    return jnp.concatenate(
        [jnp.concatenate([cos_r, -sin_r], axis=1), jnp.concatenate([sin_r, cos_r], axis=1)], axis=0
    )


def forward(signals, table, padded):
    _, blocks, _, rows = signals.shape
    half = np.arange(blocks + 1)
    cos_b, sin_b = angle_table(half, np.arange(blocks), 2 * blocks)
    first = contract("ja,sakr->sjkr", jnp.concatenate([cos_b, -sin_b]), signals)
    real, imag = first[:, : blocks + 1], first[:, blocks + 1 :]
    cos_t, sin_t = angle_table(half, np.arange(rows), padded)
    cos_t = cos_t[:, None, :]
    sin_t = sin_t[:, None, :]
    twisted = jnp.concatenate([real, imag], axis=-1) * jnp.concatenate([cos_t, cos_t], axis=-1) + jnp.concatenate(
        [imag, real], axis=-1
    ) * jnp.concatenate([sin_t, -sin_t], axis=-1)
    spectrum = jnp.einsum("rd,shkr->shkd", table, twisted, precision=PRECISION)
    return spectrum[..., :rows], spectrum[..., rows:]


def inverse(real, imag, table, padded):
    _, half_count, _, rows = real.shape
    blocks = half_count - 1
    half = np.arange(half_count)
    back = jnp.einsum(
        "rd,shkd->shkr", table, jnp.concatenate([real, imag], axis=-1), precision=PRECISION
    )
    back_real, back_imag = back[..., :rows], back[..., rows:]
    cos_t, sin_t = angle_table(half, np.arange(rows), padded)
    cos_t = cos_t[:, None, :]
    sin_t = sin_t[:, None, :]
    twisted = jnp.concatenate(
        [back_real * cos_t - back_imag * sin_t, back_imag * cos_t + back_real * sin_t], axis=1
    )
    weight = np.full(half_count, 2.0)
    weight[0] = 1.0
    weight[blocks] = 1.0
    cos_b, sin_b = angle_table(np.arange(blocks), half, 2 * blocks)
    table_b = jnp.concatenate([cos_b, -sin_b], axis=1) * jnp.asarray(np.concatenate([weight, weight]) / padded, jnp.float32)[None, :]
    return contract("ac,sckr->askr", table_b, twisted)


def prep_kernel(grad_ref, value_ref, key_ref, query_ref, filter_ref, out_ref):
    key = key_ref[...].astype(jnp.float32)
    grad_conv = (query_ref[...].astype(jnp.float32) * grad_ref[...].astype(jnp.float32)).astype(jnp.bfloat16)
    gated_value = (key * value_ref[...].astype(jnp.float32)).astype(jnp.bfloat16)
    devices, _, group, rows = out_ref.shape
    for index, block in enumerate([grad_conv, gated_value, filter_ref[...], key_ref[...]]):
        out_ref[:, index] = block.T.reshape(devices, group, rows)


def body(grad_out, value_branch, key_gate, query_gate, short_weights, long_filters):
    rows, columns = grad_out.shape[1:]
    devices = lax.axis_size("seq")
    position = lax.axis_index("seq")
    group = columns // devices
    padded = 2 * rows * devices
    send = pl.pallas_call(
        prep_kernel, out_shape=jax.ShapeDtypeStruct((devices, 4, group, rows), jnp.bfloat16)
    )(grad_out[0], value_branch[0], key_gate[0], query_gate[0], long_filters[0])
    recv = lax.all_to_all(send, "seq", split_axis=0, concat_axis=0, tiled=True)
    table = row_table(rows)
    spec_real, spec_imag = forward(jnp.swapaxes(recv[:, :3], 0, 1).astype(jnp.float32), table, padded)
    conv_real, conv_imag = spec_real[0], spec_imag[0]
    gated_real, gated_imag = spec_real[1], spec_imag[1]
    filter_real, filter_imag = spec_real[2], spec_imag[2]
    back_real = conv_real * filter_real + conv_imag * filter_imag
    back_imag = conv_imag * filter_real - conv_real * filter_imag
    fold_real = conv_real * gated_real + conv_imag * gated_imag
    fold_imag = conv_imag * gated_real - conv_real * gated_imag
    both = inverse(jnp.stack([back_real, fold_real]), jnp.stack([back_imag, fold_imag]), table, padded)
    grad_gated, grad_filter = both[:, 0], both[:, 1]
    grad_value = recv[:, 3].astype(jnp.float32) * grad_gated
    rim = jnp.concatenate(
        [grad_value[1:, :, :2], jnp.zeros((1, group, 2), grad_value.dtype)], axis=0
    )
    longer = jnp.concatenate([grad_value, rim], axis=2)
    weights = lax.dynamic_slice_in_dim(short_weights[0], position * group, group, axis=1)
    weights = weights[:, None, :, None]
    grad_input = (
        weights[0] * longer[:, :, :rows]
        + weights[1] * longer[:, :, 1 : rows + 1]
        + weights[2] * longer[:, :, 2:]
    ).astype(jnp.bfloat16)
    outgoing = jnp.stack([grad_input, grad_filter.astype(jnp.bfloat16)])
    returned = lax.all_to_all(outgoing, "seq", split_axis=1, concat_axis=1, tiled=True)
    input_tokens = returned[0].reshape(columns, rows).T
    filter_back = returned[1].astype(jnp.float32)
    filter_tokens = filter_back.reshape(columns, rows).T
    passed = shifted(input_tokens[None], "pipe", -1)
    return (passed, filter_tokens[None])


def solution(mesh):
    placed = (
        P("pipe", "seq", "chan"),
        P("pipe", "seq", "chan"),
        P("pipe", "seq", "chan"),
        P("pipe", "seq", "chan"),
        P("pipe", None, "chan"),
        P("pipe", "seq", "chan"),
    )
    return jax.shard_map(
        body,
        mesh=mesh,
        in_specs=placed,
        out_specs=(P("pipe", "seq", "chan"), P("pipe", "seq", "chan")),
        check_vma=False,
    )
```

```python
import math

import numpy as np

import jax
import jax.numpy as jnp
from jax import lax
from jax.experimental import pallas as pl
from jax.sharding import PartitionSpec as P

PRECISION = lax.Precision.HIGH


def shifted(block, axis, distance):
    devices = range(lax.axis_size(axis))
    route = [((i - distance) % len(devices), i) for i in devices]
    return lax.ppermute(block, axis, route)


def angle_table(first, second, modulus):
    first = lax.optimization_barrier(jnp.asarray(first, jnp.int32))
    products = (first[:, None] * jnp.asarray(second, jnp.int32)[None, :]) % modulus
    angles = products.astype(jnp.float32) * (2.0 * math.pi / modulus)
    return jnp.cos(angles), jnp.sin(angles)


def contract(form, table, values):
    return jnp.einsum(form, jnp.asarray(table, jnp.float32), values, precision=PRECISION)


def row_table(rows):
    index = lax.optimization_barrier(jnp.arange(rows, dtype=jnp.int32))
    angles = ((index[:, None] * index[None, :]) % rows).astype(jnp.float32) * (2.0 * math.pi / rows)
    cos_r, sin_r = jnp.cos(angles), jnp.sin(angles)
    return jnp.concatenate(
        [jnp.concatenate([cos_r, -sin_r], axis=1), jnp.concatenate([sin_r, cos_r], axis=1)], axis=0
    )


def forward(signals, table, padded):
    _, blocks, _, rows = signals.shape
    half = np.arange(blocks + 1)
    cos_b, sin_b = angle_table(half, np.arange(blocks), 2 * blocks)
    first = contract("ja,sakr->sjkr", jnp.concatenate([cos_b, -sin_b]), signals)
    real, imag = first[:, : blocks + 1], first[:, blocks + 1 :]
    cos_t, sin_t = angle_table(half, np.arange(rows), padded)
    cos_t = cos_t[:, None, :]
    sin_t = sin_t[:, None, :]
    twisted = jnp.concatenate([real * cos_t + imag * sin_t, imag * cos_t - real * sin_t], axis=-1)
    spectrum = jnp.einsum("rd,shkr->shkd", table, twisted, precision=PRECISION)
    return spectrum[..., :rows], spectrum[..., rows:]


def inverse(real, imag, table, padded):
    _, half_count, _, rows = real.shape
    blocks = half_count - 1
    half = np.arange(half_count)
    back = jnp.einsum(
        "rd,shkd->shkr", table, jnp.concatenate([real, imag], axis=-1), precision=PRECISION
    )
    back_real, back_imag = back[..., :rows], back[..., rows:]
    cos_t, sin_t = angle_table(half, np.arange(rows), padded)
    cos_t = cos_t[:, None, :]
    sin_t = sin_t[:, None, :]
    twisted = jnp.concatenate(
        [back_real * cos_t - back_imag * sin_t, back_imag * cos_t + back_real * sin_t], axis=1
    )
    weight = np.full(half_count, 2.0)
    weight[0] = 1.0
    weight[blocks] = 1.0
    cos_b, sin_b = angle_table(np.arange(blocks), half, 2 * blocks)
    table_b = jnp.concatenate([cos_b, -sin_b], axis=1) * jnp.asarray(np.concatenate([weight, weight]) / padded, jnp.float32)[None, :]
    return contract("ac,sckr->askr", table_b, twisted)


def prep_kernel(grad_ref, value_ref, key_ref, query_ref, filter_ref, out_ref):
    key = key_ref[...].astype(jnp.float32)
    grad_conv = (query_ref[...].astype(jnp.float32) * grad_ref[...].astype(jnp.float32)).astype(jnp.bfloat16)
    gated_value = (key * value_ref[...].astype(jnp.float32)).astype(jnp.bfloat16)
    devices, _, group, rows = out_ref.shape
    for index, block in enumerate([grad_conv, gated_value, filter_ref[...], key_ref[...]]):
        out_ref[:, index] = block.T.reshape(devices, group, rows)


def body(grad_out, value_branch, key_gate, query_gate, short_weights, long_filters):
    rows, columns = grad_out.shape[1:]
    devices = lax.axis_size("seq")
    position = lax.axis_index("seq")
    group = columns // devices
    padded = 2 * rows * devices
    steps = 4 if devices % 4 == 0 else 1
    width = columns // steps
    send = pl.pallas_call(
        prep_kernel,
        grid=(steps,),
        in_specs=[pl.BlockSpec((rows, width), lambda i: (0, i))] * 5,
        out_specs=pl.BlockSpec((devices // steps, 4, group, rows), lambda i: (i, 0, 0, 0)),
        out_shape=jax.ShapeDtypeStruct((devices, 4, group, rows), jnp.bfloat16),
    )(grad_out[0], value_branch[0], key_gate[0], query_gate[0], long_filters[0])
    recv = lax.all_to_all(send, "seq", split_axis=0, concat_axis=0, tiled=True)
    table = row_table(rows)
    spec_real, spec_imag = forward(jnp.swapaxes(recv[:, :3], 0, 1).astype(jnp.float32), table, padded)
    conv_real, conv_imag = spec_real[0], spec_imag[0]
    gated_real, gated_imag = spec_real[1], spec_imag[1]
    filter_real, filter_imag = spec_real[2], spec_imag[2]
    back_real = conv_real * filter_real + conv_imag * filter_imag
    back_imag = conv_imag * filter_real - conv_real * filter_imag
    fold_real = conv_real * gated_real + conv_imag * gated_imag
    fold_imag = conv_imag * gated_real - conv_real * gated_imag
    both = inverse(jnp.stack([back_real, fold_real]), jnp.stack([back_imag, fold_imag]), table, padded)
    grad_gated, grad_filter = both[:, 0], both[:, 1]
    grad_value = recv[:, 3].astype(jnp.float32) * grad_gated
    rim = jnp.concatenate(
        [grad_value[1:, :, :2], jnp.zeros((1, group, 2), grad_value.dtype)], axis=0
    )
    longer = jnp.concatenate([grad_value, rim], axis=2)
    weights = lax.dynamic_slice_in_dim(short_weights[0], position * group, group, axis=1)
    weights = weights[:, None, :, None]
    grad_input = (
        weights[0] * longer[:, :, :rows]
        + weights[1] * longer[:, :, 1 : rows + 1]
        + weights[2] * longer[:, :, 2:]
    ).astype(jnp.bfloat16)
    outgoing = jnp.stack([grad_input, grad_filter.astype(jnp.bfloat16)])
    returned = lax.all_to_all(outgoing, "seq", split_axis=1, concat_axis=1, tiled=True)
    input_tokens = returned[0].reshape(columns, rows).T
    filter_back = returned[1].astype(jnp.float32)
    filter_tokens = filter_back.reshape(columns, rows).T
    passed = shifted(input_tokens[None], "pipe", -1)
    return (passed, filter_tokens[None])


def solution(mesh):
    placed = (
        P("pipe", "seq", "chan"),
        P("pipe", "seq", "chan"),
        P("pipe", "seq", "chan"),
        P("pipe", "seq", "chan"),
        P("pipe", None, "chan"),
        P("pipe", "seq", "chan"),
    )
    return jax.shard_map(
        body,
        mesh=mesh,
        in_specs=placed,
        out_specs=(P("pipe", "seq", "chan"), P("pipe", "seq", "chan")),
        check_vma=False,
    )
```

```python
import math

import numpy as np

import jax
import jax.numpy as jnp
from jax import lax
from jax.experimental import pallas as pl
from jax.sharding import PartitionSpec as P

PRECISION = lax.Precision.HIGH


def shifted(block, axis, distance):
    devices = range(lax.axis_size(axis))
    route = [((i - distance) % len(devices), i) for i in devices]
    return lax.ppermute(block, axis, route)


def angle_table(first, second, modulus):
    first = lax.optimization_barrier(jnp.asarray(first, jnp.int32))
    products = (first[:, None] * jnp.asarray(second, jnp.int32)[None, :]) % modulus
    angles = products.astype(jnp.float32) * (2.0 * math.pi / modulus)
    return jnp.cos(angles), jnp.sin(angles)


def contract(form, table, values):
    return jnp.einsum(form, jnp.asarray(table, jnp.float32), values, precision=PRECISION)


def row_table(rows):
    index = lax.optimization_barrier(jnp.arange(rows, dtype=jnp.int32))
    angles = ((index[:, None] * index[None, :]) % rows).astype(jnp.float32) * (2.0 * math.pi / rows)
    cos_r, sin_r = jnp.cos(angles), jnp.sin(angles)
    return jnp.concatenate(
        [jnp.concatenate([cos_r, -sin_r], axis=1), jnp.concatenate([sin_r, cos_r], axis=1)], axis=0
    )


def forward(signals, table, padded):
    _, blocks, _, rows = signals.shape
    half = np.arange(blocks + 1)
    cos_b, sin_b = angle_table(half, np.arange(blocks), 2 * blocks)
    first = contract("ja,sakr->sjkr", jnp.concatenate([cos_b, -sin_b]), signals)
    real, imag = first[:, : blocks + 1], first[:, blocks + 1 :]
    cos_t, sin_t = angle_table(half, np.arange(rows), padded)
    cos_t = cos_t[:, None, :]
    sin_t = sin_t[:, None, :]
    twisted = jnp.concatenate([real * cos_t + imag * sin_t, imag * cos_t - real * sin_t], axis=-1)
    spectrum = jnp.einsum("rd,shkr->shkd", table, twisted, precision=PRECISION)
    return spectrum[..., :rows], spectrum[..., rows:]


def inverse(real, imag, table, padded):
    _, half_count, _, rows = real.shape
    blocks = half_count - 1
    half = np.arange(half_count)
    back = jnp.einsum(
        "rd,shkd->shkr", table, jnp.concatenate([real, imag], axis=-1), precision=PRECISION
    )
    back_real, back_imag = back[..., :rows], back[..., rows:]
    cos_t, sin_t = angle_table(half, np.arange(rows), padded)
    cos_t = cos_t[:, None, :]
    sin_t = sin_t[:, None, :]
    twisted = jnp.concatenate([back_real, back_imag], axis=1) * jnp.concatenate(
        [cos_t, cos_t], axis=0
    ) + jnp.concatenate([back_imag, back_real], axis=1) * jnp.concatenate([-sin_t, sin_t], axis=0)
    weight = np.full(half_count, 2.0)
    weight[0] = 1.0
    weight[blocks] = 1.0
    cos_b, sin_b = angle_table(np.arange(blocks), half, 2 * blocks)
    table_b = jnp.concatenate([cos_b, -sin_b], axis=1) * jnp.asarray(np.concatenate([weight, weight]) / padded, jnp.float32)[None, :]
    return contract("ac,sckr->askr", table_b, twisted)


def prep_kernel(grad_ref, value_ref, key_ref, query_ref, filter_ref, out_ref):
    key = key_ref[...].astype(jnp.float32)
    grad_conv = (query_ref[...].astype(jnp.float32) * grad_ref[...].astype(jnp.float32)).astype(jnp.bfloat16)
    gated_value = (key * value_ref[...].astype(jnp.float32)).astype(jnp.bfloat16)
    devices, _, group, rows = out_ref.shape
    for index, block in enumerate([grad_conv, gated_value, filter_ref[...], key_ref[...]]):
        out_ref[:, index] = block.T.reshape(devices, group, rows)


def body(grad_out, value_branch, key_gate, query_gate, short_weights, long_filters):
    rows, columns = grad_out.shape[1:]
    devices = lax.axis_size("seq")
    position = lax.axis_index("seq")
    group = columns // devices
    padded = 2 * rows * devices
    send = pl.pallas_call(
        prep_kernel, out_shape=jax.ShapeDtypeStruct((devices, 4, group, rows), jnp.bfloat16)
    )(grad_out[0], value_branch[0], key_gate[0], query_gate[0], long_filters[0])
    recv = lax.all_to_all(send, "seq", split_axis=0, concat_axis=0, tiled=True)
    table = row_table(rows)
    spec_real, spec_imag = forward(jnp.swapaxes(recv[:, :3], 0, 1).astype(jnp.float32), table, padded)
    conv_real, conv_imag = spec_real[0], spec_imag[0]
    gated_real, gated_imag = spec_real[1], spec_imag[1]
    filter_real, filter_imag = spec_real[2], spec_imag[2]
    back_real = conv_real * filter_real + conv_imag * filter_imag
    back_imag = conv_imag * filter_real - conv_real * filter_imag
    fold_real = conv_real * gated_real + conv_imag * gated_imag
    fold_imag = conv_imag * gated_real - conv_real * gated_imag
    both = inverse(jnp.stack([back_real, fold_real]), jnp.stack([back_imag, fold_imag]), table, padded)
    grad_gated, grad_filter = both[:, 0], both[:, 1]
    grad_value = recv[:, 3].astype(jnp.float32) * grad_gated
    rim = jnp.concatenate(
        [grad_value[1:, :, :2], jnp.zeros((1, group, 2), grad_value.dtype)], axis=0
    )
    longer = jnp.concatenate([grad_value, rim], axis=2)
    weights = lax.dynamic_slice_in_dim(short_weights[0], position * group, group, axis=1)
    weights = weights[:, None, :, None]
    grad_input = (
        weights[0] * longer[:, :, :rows]
        + weights[1] * longer[:, :, 1 : rows + 1]
        + weights[2] * longer[:, :, 2:]
    ).astype(jnp.bfloat16)
    outgoing = jnp.stack([grad_input, grad_filter.astype(jnp.bfloat16)])
    returned = lax.all_to_all(outgoing, "seq", split_axis=1, concat_axis=1, tiled=True)
    input_tokens = returned[0].reshape(columns, rows).T
    filter_back = returned[1].astype(jnp.float32)
    filter_tokens = filter_back.reshape(columns, rows).T
    passed = shifted(input_tokens[None], "pipe", -1)
    return (passed, filter_tokens[None])


def solution(mesh):
    placed = (
        P("pipe", "seq", "chan"),
        P("pipe", "seq", "chan"),
        P("pipe", "seq", "chan"),
        P("pipe", "seq", "chan"),
        P("pipe", None, "chan"),
        P("pipe", "seq", "chan"),
    )
    return jax.shard_map(
        body,
        mesh=mesh,
        in_specs=placed,
        out_specs=(P("pipe", "seq", "chan"), P("pipe", "seq", "chan")),
        check_vma=False,
    )
```
